512 devices in a mesh: cell: 64 (over z, y), tm: 8 (over x, core).
Axes of the slice: x: 4, y: 8, z: 8, core: 2. Of those that a mesh axis runs over, the one named last changes fastest.
Arguments:
- flux: bfloat16 [32, 16, 32768], P('tm', None, 'cell'), may hold values from -6 to 6
- foot: bfloat16 [4096, 64, 128], P('cell', 'tm'), may hold values from 0 to 0.029907227
- block_slot: int32 [4096, 64], P('cell', 'tm'), may hold values from 0 to 127, as said below
- block_time: int32 [4096, 64], P('cell', 'tm'), may hold values from 0 to 3
- block_count: int32 [4096, 8], P('cell', 'tm'), may hold values from 1 to 8, as said below
- request_tiles: int32 [64, 64, 2], P('cell'), may hold values from 0 to 3
- obs_weight: float32 [4096], P('cell'), may hold values from 1 to 10
- prior: float32 [32, 32], replicated
Outputs:
- obs_image: float32 [4096, 16], P('cell')
- hess: float32 [32, 16, 32768], P('tm', None, 'cell')
The draws below stay inside these ranges and needn't reach their ends.
Inputs may be any that keep to these rules, and one draw needn't show every extreme that they name: `block_count`: every index along cell holds a sounding with 8 live blocks in every time group. Among the blocks of one device (its 64 soundings' slots of one time group), one source block_slot // 2 is named by exactly 16 blocks and no source by more.
All inputs are finite; a program needn't handle non-finite values.
Results may differ from the reference program's by a relative error of at most 0.00085.
Values may be sent and summed in bfloat16 or wider, within the bound.
No kernel may reach another device: no remote copies, remote signals or barrier semaphores. Data moves between devices by JAX's collectives and lax.ppermute only.
A program may use at most 64 MiB of HBM per device.

```python
import math
import jax
import jax.numpy as jnp
from jax import lax

K = 16
TILE = 128
TILES_DEV = 4
TSL_DEV = 4
S_DEV = 64
NB_DEV = 8
CAP = 2
CELLS = 32768
T_ALL = 32
SOUND = 4096
NB_TOT = 64
SOURCES = 64
N_CELL = 64
N_TM = 8


def draw_block_count(key, part):
    key_level = jax.random.fold_in(key, 11)
    key_value = jax.random.fold_in(key, 12)
    level = jax.random.randint(key_level, (N_CELL,), 2, NB_DEV + 1)
    raw_value = jax.random.randint(key_value, (SOUND, N_TM), 0, NB_DEV)
    level_row = jnp.repeat(level, S_DEV)[:, None]
    counts = 1 + raw_value % level_row
    first_row = (jnp.arange(SOUND) % S_DEV == 0)[:, None]
    return jnp.where(first_row, NB_DEV, counts).astype(jnp.int32)


def draw_block_slot(key, part):
    dev_blocks = S_DEV * NB_DEV
    most_blocks = max(2, 2 * dev_blocks // N_CELL)
    base_key = jax.random.fold_in(key, 21)

    def one_device(index):
        device_key = jax.random.fold_in(base_key, index)
        hot_source = jax.random.randint(jax.random.fold_in(device_key, 1), (), 0, N_CELL)
        counter = jnp.arange(dev_blocks, dtype=jnp.int32)
        others = (hot_source + 1 + (counter - most_blocks) % (N_CELL - 1)) % N_CELL
        source = jnp.where(counter < most_blocks, hot_source, others)
        source = jax.random.permutation(jax.random.fold_in(device_key, 2), source)
        position = jax.random.randint(jax.random.fold_in(device_key, 3), (dev_blocks,), 0, CAP)
        return (source * CAP + position).astype(jnp.int32)
    table = jax.vmap(one_device)(jnp.arange(N_CELL * N_TM, dtype=jnp.int32))
    table = table.reshape(N_CELL, N_TM, S_DEV, NB_DEV).transpose(0, 2, 1, 3)
    return table.reshape(SOUND, NB_TOT).astype(jnp.int32)


def draw_prior(key, part):
    noise = jax.random.normal(key, (T_ALL, T_ALL), jnp.float32)
    return jnp.eye(T_ALL, dtype=jnp.float32) * 1.5 + noise * (0.6 / T_ALL ** 0.5)


def place_ends(drawn, own_key, low, top_value):
    dims = drawn.shape
    place = [jax.random.randint(jax.random.fold_in(own_key, axis), (), 0, dims[axis]) for axis in range(len(dims))]
    drawn = drawn.at[tuple(place)].set(low)
    longest = dims.index(max(dims))
    place[longest] = (place[longest] + 1) % dims[longest]
    return drawn.at[tuple(place)].set(top_value)


def level_of(own_key, extent, shards, smallest, largest):
    factor_of = 1.0
    for dim, shards_of in shards:
        heights = jax.random.uniform(jax.random.fold_in(jax.random.fold_in(own_key, 6), dim), (shards_of,), jnp.float32, smallest / len(shards), largest / len(shards))
        factor_of = factor_of * jnp.repeat(jnp.exp(heights), extent[dim] // shards_of).reshape((-1,) + (1,) * (len(extent) - 1 - dim))
    return factor_of


def normal_values(own_key, extent, width, limit, cuts=(), held_as=jnp.bfloat16):
    values = jax.random.normal(own_key, extent, jnp.float32) * width
    if len(cuts) > 0:
        values = level_of(own_key, extent, cuts, -0.22, 0.18) * values
    return jnp.clip(values, min=-limit, max=limit).astype(held_as)


def setup_inputs(seed: int = 0) -> dict:
    key_list = jax.random.split(jax.random.key(seed), 9)
    return {
        "flux": normal_values(key_list[0], (T_ALL, K, CELLS), 1.0, 6.0, ((0, 8), (2, 64))),
        "foot": jnp.clip(0.029907227 * jax.random.uniform(key_list[1], (SOUND, NB_TOT, TILE), jnp.float32) ** level_of(key_list[1], (SOUND, NB_TOT, TILE), ((0, 64), (1, 8)), -0.2, 0.2), 0.0, 0.029907227).astype(jnp.bfloat16),
        "block_slot": draw_block_slot(jax.random.fold_in(key_list[8], 71), 0),
        "block_time": place_ends(jax.random.randint(key_list[3], (SOUND, NB_TOT), 0, TSL_DEV), jax.random.fold_in(key_list[3], 1), 0, TSL_DEV - 1).astype(jnp.int32),
        "block_count": draw_block_count(jax.random.fold_in(key_list[8], 71), 0),
        "request_tiles": place_ends(jax.random.randint(key_list[5], (SOURCES, SOURCES, CAP), 0, TILES_DEV), jax.random.fold_in(key_list[5], 1), 0, TILES_DEV - 1).astype(jnp.int32),
        "obs_weight": jnp.clip(jnp.exp(math.log(10.0) - 2.3025851 * jax.random.uniform(key_list[6], (SOUND,), jnp.float32) ** level_of(key_list[6], (SOUND,), ((0, 64),), -0.2, 0.2)), 1.0, 10.0),
        "prior": draw_prior(jax.random.fold_in(key_list[8], 71), 0),
    }


def locate(owner, slot_ids, time_ids, count_ids, request_tiles):
    blocks = slot_ids.shape[1]
    group_of = jnp.arange(blocks, dtype=jnp.int32) // NB_DEV
    source = slot_ids // CAP
    position = slot_ids % CAP
    global_tile = source * TILES_DEV + request_tiles[owner, source, position]
    global_time = group_of[None, :] * TSL_DEV + time_ids
    block_live = (jnp.arange(blocks, dtype=jnp.int32) % NB_DEV)[None, :] < count_ids[:, group_of]
    return global_tile.astype(jnp.int32), global_time.astype(jnp.int32), block_live


def reference(flux, foot, block_slot, block_time, block_count, request_tiles, obs_weight, prior):
    slices, directions, cell_count = flux.shape
    blocks = foot.shape[1]
    tiled = flux.astype(jnp.float32).reshape(slices, directions, cell_count // TILE, TILE)
    owners = jnp.arange(N_CELL, dtype=jnp.int32)
    foot_dev = foot.reshape(N_CELL, S_DEV, blocks, TILE)
    slot_dev = block_slot.reshape(N_CELL, S_DEV, blocks)
    time_dev = block_time.reshape(N_CELL, S_DEV, blocks)
    count_dev = block_count.reshape(N_CELL, S_DEV, N_TM)

    def forward(inputs):
        owner, weights, slot_ids, time_ids, count_ids = inputs
        global_tile, global_time, block_live = locate(owner, slot_ids, time_ids, count_ids, request_tiles)
        picked = tiled[global_time, :, global_tile, :]
        masked = jnp.where(block_live[:, :, None], weights.astype(jnp.float32), jnp.float32(0.0))
        return jnp.einsum("sjc,sjkc->sk", masked, picked)

    obs_image = lax.map(forward, (owners, foot_dev, slot_dev, time_dev, count_dev)).reshape(SOUND, directions)
    weighted = obs_weight[:, None] * obs_image
    weighted_dev = weighted.reshape(N_CELL, S_DEV, directions)

    def backward(running, inputs):
        owner, weights, slot_ids, time_ids, count_ids, scaled = inputs
        global_tile, global_time, block_live = locate(owner, slot_ids, time_ids, count_ids, request_tiles)
        masked = jnp.where(block_live[:, :, None], weights.astype(jnp.float32), jnp.float32(0.0))
        update = masked[:, :, None, :] * scaled[:, None, :, None]
        return running.at[global_time, :, global_tile, :].add(update), None

    start_sum = jnp.zeros((slices, directions, cell_count // TILE, TILE), jnp.float32)
    adjoint, _ = lax.scan(backward, start_sum, (owners, foot_dev, slot_dev, time_dev, count_dev, weighted_dev))
    coupled = jnp.einsum("ts,skn->tkn", prior, flux.astype(jnp.float32), precision=lax.Precision.HIGHEST)
    hess = adjoint.reshape(slices, directions, cell_count) + coupled
    return obs_image, hess
```

```python
import jax
import jax.numpy as jnp
from jax import lax
from jax.sharding import PartitionSpec as P

TILE = 128
HI = lax.Precision.HIGHEST


def local(flux, foot, block_slot, block_time, block_count, request_tiles, obs_weight, prior):
    slices, directions, cell_count = flux.shape
    tiles = cell_count // TILE
    sounds, nb, _ = foot.shape
    n_source = request_tiles.shape[1]
    per_source = request_tiles.shape[2]
    n_blocks = sounds * nb
    cap = 16
    n_slot = n_source * cap
    n_meta = tiles * slices
    f32 = jnp.float32

    live = (jnp.arange(nb, dtype=jnp.int32)[None, :] < block_count).reshape(n_blocks)
    slot_ids = block_slot.reshape(n_blocks)
    source = slot_ids // per_source
    position = slot_ids % per_source
    local_tile = request_tiles[0].reshape(n_source * per_source)[source * per_source + position]
    meta = local_tile * slices + block_time.reshape(n_blocks)
    src_hot = (source[:, None] == jnp.arange(n_source, dtype=jnp.int32)[None, :]) & live[:, None]
    src_hot_b = src_hot.astype(jnp.bfloat16)
    row = jnp.arange(n_blocks, dtype=jnp.int32)
    lower = (row[None, :] < row[:, None]).astype(jnp.bfloat16)
    before = jnp.dot(lower, src_hot_b, preferred_element_type=f32)
    rank = jnp.sum(before * src_hot_b.astype(f32), axis=1).astype(jnp.int32)
    dest = jnp.where(live, source * cap + rank, n_slot)
    place = (dest[None, :] == jnp.arange(n_slot, dtype=jnp.int32)[:, None])
    place_b = place.astype(jnp.bfloat16)
    foot_flat = foot.reshape(n_blocks, TILE)
    foot_send = jnp.dot(place_b, foot_flat, preferred_element_type=f32).astype(jnp.bfloat16)
    meta_send = jnp.dot(place_b, meta.astype(jnp.bfloat16)[:, None], preferred_element_type=f32)
    meta_send = meta_send.reshape(n_source, cap).astype(jnp.bfloat16)
    meta_pad = jnp.zeros((n_source, TILE - cap), jnp.bfloat16)
    send = jnp.concatenate([foot_send.reshape(n_source, cap * TILE), meta_send, meta_pad], axis=1)
    recv = lax.all_to_all(send, "cell", split_axis=0, concat_axis=0, tiled=True)

    foot_r = recv[:, : cap * TILE].reshape(n_slot, TILE)
    meta_r = recv[:, cap * TILE : cap * TILE + cap].reshape(n_slot).astype(jnp.int32)
    meta_hot = (meta_r[:, None] == jnp.arange(n_meta, dtype=jnp.int32)[None, :]).astype(f32)
    panels = flux.reshape(slices, directions, tiles, TILE).transpose(3, 2, 0, 1)
    panels = panels.reshape(TILE, n_meta * directions)
    every = jnp.dot(foot_r, panels, preferred_element_type=f32).reshape(n_slot, n_meta, directions)
    partial = jnp.sum(every * meta_hot[:, :, None], axis=1)
    back = lax.all_to_all(
        partial.reshape(n_source, cap * directions), "cell", split_axis=0, concat_axis=0, tiled=True
    ).reshape(n_slot, directions)

    place_f = place.astype(f32)
    per_block = jnp.dot(place_f.T, back, precision=HI, preferred_element_type=f32)
    partial_value = per_block.reshape(sounds, nb, directions).sum(axis=1)
    images = lax.psum(partial_value, "tm")
    weighted = obs_weight[:, None] * images
    w_block = jnp.repeat(weighted, nb, axis=0)
    w_send = jnp.dot(place_f, w_block, precision=HI, preferred_element_type=f32)
    w_recv = lax.all_to_all(
        w_send.reshape(n_source, cap * directions), "cell", split_axis=0, concat_axis=0, tiled=True
    ).reshape(n_slot, directions)

    w_meta = (meta_hot[:, :, None] * w_recv[:, None, :]).reshape(n_slot, n_meta * directions)
    adj = jnp.dot(w_meta.T, foot_r.astype(f32), precision=HI, preferred_element_type=f32)
    adj = adj.reshape(tiles, slices, directions, TILE).transpose(1, 2, 0, 3)
    adjoint = adj.reshape(slices, directions, cell_count)

    my_group = lax.axis_index("tm")
    flux_wide = flux.astype(f32)
    panel = lax.dynamic_slice(prior, (0, my_group * slices), (lax.axis_size("tm") * slices, slices))
    coupled = lax.psum_scatter(
        jnp.einsum("ts,skn->tkn", panel, flux_wide, precision=HI),
        "tm",
        scatter_dimension=0,
        tiled=True,
    )
    hess = adjoint + coupled
    return (images, hess)


def solution(mesh):
    in_specs = (
        P("tm", None, "cell"),
        P("cell", "tm", None),
        P("cell", "tm"),
        P("cell", "tm"),
        P("cell", "tm"),
        P("cell", None, None),
        P("cell"),
        P(),
    )
    out_specs = (P("cell", None), P("tm", None, "cell"))
    return jax.shard_map(local, mesh=mesh, in_specs=in_specs, out_specs=out_specs, check_vma=False)
```

```python
import jax
import jax.numpy as jnp
from jax import lax
from jax.sharding import PartitionSpec as P

TILE = 128
HI = lax.Precision.HIGHEST


def local(flux, foot, block_slot, block_time, block_count, request_tiles, obs_weight, prior):
    slices, directions, cell_count = flux.shape
    tiles = cell_count // TILE
    sounds, nb, _ = foot.shape
    n_source = request_tiles.shape[1]
    per_source = request_tiles.shape[2]
    n_blocks = sounds * nb
    cap = 16
    n_slot = n_source * cap
    n_meta = tiles * slices
    f32 = jnp.float32

    live = (jnp.arange(nb, dtype=jnp.int32)[None, :] < block_count).reshape(n_blocks)
    slot_ids = block_slot.reshape(n_blocks)
    source = slot_ids // per_source
    position = slot_ids % per_source
    table = request_tiles[0].reshape(n_source * per_source)
    pick = slot_ids[:, None] == jnp.arange(n_source * per_source, dtype=jnp.int32)[None, :]
    local_tile = jnp.sum(jnp.where(pick, table[None, :], 0), axis=1)
    meta = local_tile * slices + block_time.reshape(n_blocks)
    src_hot = (source[:, None] == jnp.arange(n_source, dtype=jnp.int32)[None, :]) & live[:, None]
    src_hot_b = src_hot.astype(jnp.bfloat16)
    row = jnp.arange(n_blocks, dtype=jnp.int32)
    lower = (row[None, :] < row[:, None]).astype(jnp.bfloat16)
    before = jnp.dot(lower, src_hot_b, preferred_element_type=f32)
    rank = jnp.sum(before * src_hot_b.astype(f32), axis=1).astype(jnp.int32)
    dest = jnp.where(live, source * cap + rank, n_slot)
    place = (dest[None, :] == jnp.arange(n_slot, dtype=jnp.int32)[:, None])
    place_b = place.astype(jnp.bfloat16)
    foot_flat = foot.reshape(n_blocks, TILE)
    foot_send = jnp.dot(place_b, foot_flat, preferred_element_type=f32).astype(jnp.bfloat16)
    meta_send = jnp.dot(place_b, meta.astype(jnp.bfloat16)[:, None], preferred_element_type=f32)
    meta_send = meta_send.reshape(n_source, cap).astype(jnp.bfloat16)
    meta_pad = jnp.zeros((n_source, TILE - cap), jnp.bfloat16)
    send = jnp.concatenate([foot_send.reshape(n_source, cap * TILE), meta_send, meta_pad], axis=1)
    recv = lax.all_to_all(send, "cell", split_axis=0, concat_axis=0, tiled=True)

    foot_r = recv[:, : cap * TILE].reshape(n_slot, TILE)
    meta_r = recv[:, cap * TILE : cap * TILE + cap].reshape(n_slot).astype(jnp.int32)
    meta_hot = (meta_r[:, None] == jnp.arange(n_meta, dtype=jnp.int32)[None, :]).astype(f32)
    panels = flux.reshape(slices, directions, tiles, TILE).transpose(3, 2, 0, 1)
    panels = panels.reshape(TILE, n_meta * directions)
    every = jnp.dot(foot_r, panels, preferred_element_type=f32).reshape(n_slot, n_meta, directions)
    partial = jnp.sum(every * meta_hot[:, :, None], axis=1)
    back = lax.all_to_all(
        partial.reshape(n_source, cap * directions), "cell", split_axis=0, concat_axis=0, tiled=True
    ).reshape(n_slot, directions)

    place_f = place.astype(f32)
    per_block = jnp.dot(place_f.T, back, precision=HI, preferred_element_type=f32)
    partial_value = per_block.reshape(sounds, nb, directions).sum(axis=1)
    images = lax.psum(partial_value, "tm")
    weighted = obs_weight[:, None] * images
    w_block = jnp.repeat(weighted, nb, axis=0)
    w_send = jnp.dot(place_f, w_block, precision=HI, preferred_element_type=f32)
    w_recv = lax.all_to_all(
        w_send.reshape(n_source, cap * directions), "cell", split_axis=0, concat_axis=0, tiled=True
    ).reshape(n_slot, directions)

    w_meta = (meta_hot[:, :, None] * w_recv[:, None, :]).reshape(n_slot, n_meta * directions)
    adj = jnp.dot(w_meta.T, foot_r.astype(f32), precision=HI, preferred_element_type=f32)
    adj = adj.reshape(tiles, slices, directions, TILE).transpose(1, 2, 0, 3)
    adjoint = adj.reshape(slices, directions, cell_count)

    my_group = lax.axis_index("tm")
    groups = lax.axis_size("tm")
    copies = jnp.broadcast_to(flux[None], (groups,) + flux.shape)
    flux_all = lax.all_to_all(copies, "tm", split_axis=0, concat_axis=0, tiled=True)
    flux_all = flux_all.reshape(groups * slices, directions, cell_count).astype(f32)
    panel = lax.dynamic_slice(prior, (my_group * slices, 0), (slices, groups * slices))
    coupled = jnp.einsum("ts,skn->tkn", panel, flux_all, precision=HI)
    hess = adjoint + coupled
    return (images, hess)


def solution(mesh):
    in_specs = (
        P("tm", None, "cell"),
        P("cell", "tm", None),
        P("cell", "tm"),
        P("cell", "tm"),
        P("cell", "tm"),
        P("cell", None, None),
        P("cell"),
        P(),
    )
    out_specs = (P("cell", None), P("tm", None, "cell"))
    return jax.shard_map(local, mesh=mesh, in_specs=in_specs, out_specs=out_specs, check_vma=False)
```

```python
import jax
import jax.numpy as jnp
from jax import lax
from jax.sharding import PartitionSpec as P

TILE = 128
HI = lax.Precision.HIGHEST


def local(flux, foot, block_slot, block_time, block_count, request_tiles, obs_weight, prior):
    slices, directions, cell_count = flux.shape
    tiles = cell_count // TILE
    sounds, nb, _ = foot.shape
    n_source = request_tiles.shape[1]
    per_source = request_tiles.shape[2]
    n_blocks = sounds * nb
    cap = 16
    n_slot = n_source * cap
    n_meta = tiles * slices
    f32 = jnp.float32

    live = (jnp.arange(nb, dtype=jnp.int32)[None, :] < block_count).reshape(n_blocks)
    slot_ids = block_slot.reshape(n_blocks)
    source = slot_ids // per_source
    position = slot_ids % per_source
    table = request_tiles[0].reshape(n_source * per_source)
    pick = slot_ids[:, None] == jnp.arange(n_source * per_source, dtype=jnp.int32)[None, :]
    local_tile = jnp.sum(jnp.where(pick, table[None, :], 0), axis=1)
    meta = local_tile * slices + block_time.reshape(n_blocks)
    src_hot = (source[:, None] == jnp.arange(n_source, dtype=jnp.int32)[None, :]) & live[:, None]
    src_hot_b = src_hot.astype(jnp.bfloat16)
    row = jnp.arange(n_blocks, dtype=jnp.int32)
    lower = (row[None, :] < row[:, None]).astype(jnp.bfloat16)
    before = jnp.dot(lower, src_hot_b, preferred_element_type=f32)
    rank = jnp.sum(before * src_hot_b.astype(f32), axis=1).astype(jnp.int32)
    dest = jnp.where(live, source * cap + rank, n_slot)
    place = (dest[None, :] == jnp.arange(n_slot, dtype=jnp.int32)[:, None])
    place_b = place.astype(jnp.bfloat16)
    foot_flat = foot.reshape(n_blocks, TILE)
    foot_send = jnp.dot(place_b, foot_flat, preferred_element_type=f32).astype(jnp.bfloat16)
    meta_send = jnp.dot(place_b, meta.astype(jnp.bfloat16)[:, None], preferred_element_type=f32)
    meta_send = meta_send.reshape(n_source, cap).astype(jnp.bfloat16)
    meta_pad = jnp.zeros((n_source, TILE - cap), jnp.bfloat16)
    send = jnp.concatenate([foot_send.reshape(n_source, cap * TILE), meta_send, meta_pad], axis=1)
    recv = lax.all_to_all(send, "cell", split_axis=0, concat_axis=0, tiled=True)

    my_group = lax.axis_index("tm")
    groups = lax.axis_size("tm")
    copies = jnp.broadcast_to(flux[None], (groups,) + flux.shape)
    flux_all = lax.all_to_all(copies, "tm", split_axis=0, concat_axis=0, tiled=True)
    flux_all = flux_all.reshape(groups * slices, directions, cell_count).astype(f32)

    foot_r = recv[:, : cap * TILE].reshape(n_slot, TILE)
    meta_r = recv[:, cap * TILE : cap * TILE + cap].reshape(n_slot).astype(jnp.int32)
    meta_hot = (meta_r[:, None] == jnp.arange(n_meta, dtype=jnp.int32)[None, :]).astype(f32)
    panels = flux.reshape(slices, directions, tiles, TILE).transpose(3, 2, 0, 1)
    panels = panels.reshape(TILE, n_meta * directions)
    every = jnp.dot(foot_r, panels, preferred_element_type=f32).reshape(n_slot, n_meta, directions)
    partial = jnp.sum(every * meta_hot[:, :, None], axis=1)
    flux_all, partial = lax.optimization_barrier((flux_all, partial))
    back = lax.all_to_all(
        partial.reshape(n_source, cap * directions), "cell", split_axis=0, concat_axis=0, tiled=True
    ).reshape(n_slot, directions)

    place_f = place.astype(f32)
    per_block = jnp.dot(place_f.T, back, precision=HI, preferred_element_type=f32)
    partial_value = per_block.reshape(sounds, nb, directions).sum(axis=1)
    images = lax.psum(partial_value, "tm")
    weighted = obs_weight[:, None] * images
    w_block = jnp.repeat(weighted, nb, axis=0)
    w_send = jnp.dot(place_f, w_block, precision=HI, preferred_element_type=f32)
    w_recv = lax.all_to_all(
        w_send.reshape(n_source, cap * directions), "cell", split_axis=0, concat_axis=0, tiled=True
    ).reshape(n_slot, directions)

    w_meta = (meta_hot[:, :, None] * w_recv[:, None, :]).reshape(n_slot, n_meta * directions)
    adj = jnp.dot(w_meta.T, foot_r.astype(f32), precision=HI, preferred_element_type=f32)
    adj = adj.reshape(tiles, slices, directions, TILE).transpose(1, 2, 0, 3)
    adjoint = adj.reshape(slices, directions, cell_count)

    panel = lax.dynamic_slice(prior, (my_group * slices, 0), (slices, groups * slices))
    coupled = jnp.einsum("ts,skn->tkn", panel, flux_all, precision=HI)
    hess = adjoint + coupled
    return (images, hess)


def solution(mesh):
    in_specs = (
        P("tm", None, "cell"),
        P("cell", "tm", None),
        P("cell", "tm"),
        P("cell", "tm"),
        P("cell", "tm"),
        P("cell", None, None),
        P("cell"),
        P(),
    )
    out_specs = (P("cell", None), P("tm", None, "cell"))
    return jax.shard_map(local, mesh=mesh, in_specs=in_specs, out_specs=out_specs, check_vma=False)
```

```python
import jax
import jax.numpy as jnp
from jax import lax
from jax.sharding import PartitionSpec as P

TILE = 128
HI = lax.Precision.HIGHEST


def local(flux, foot, block_slot, block_time, block_count, request_tiles, obs_weight, prior):
    slices, directions, cell_count = flux.shape
    tiles = cell_count // TILE
    sounds, nb, _ = foot.shape
    n_source = request_tiles.shape[1]
    per_source = request_tiles.shape[2]
    n_blocks = sounds * nb
    cap = 16
    n_slot = n_source * cap
    n_meta = tiles * slices
    f32 = jnp.float32

    live = (jnp.arange(nb, dtype=jnp.int32)[None, :] < block_count).reshape(n_blocks)
    slot_ids = block_slot.reshape(n_blocks)
    source = slot_ids // per_source
    position = slot_ids % per_source
    table = request_tiles[0].reshape(n_source * per_source)
    pick = slot_ids[:, None] == jnp.arange(n_source * per_source, dtype=jnp.int32)[None, :]
    local_tile = jnp.sum(jnp.where(pick, table[None, :], 0), axis=1)
    meta = local_tile * slices + block_time.reshape(n_blocks)
    src_hot = (source[:, None] == jnp.arange(n_source, dtype=jnp.int32)[None, :]) & live[:, None]
    src_hot_b = src_hot.astype(jnp.bfloat16)
    row = jnp.arange(n_blocks, dtype=jnp.int32)
    lower = (row[None, :] < row[:, None]).astype(jnp.bfloat16)
    before = jnp.dot(lower, src_hot_b, preferred_element_type=f32)
    rank = jnp.sum(before * src_hot_b.astype(f32), axis=1).astype(jnp.int32)
    dest = jnp.where(live, source * cap + rank, n_slot)
    place = (dest[None, :] == jnp.arange(n_slot, dtype=jnp.int32)[:, None])
    place_b = place.astype(jnp.bfloat16)
    foot_flat = foot.reshape(n_blocks, TILE)
    foot_send = jnp.dot(place_b, foot_flat, preferred_element_type=f32).astype(jnp.bfloat16)
    meta_send = jnp.dot(place_b, meta.astype(jnp.bfloat16)[:, None], preferred_element_type=f32)
    meta_send = meta_send.reshape(n_source, cap).astype(jnp.bfloat16)
    meta_pad = jnp.zeros((n_source, TILE - cap), jnp.bfloat16)
    send = jnp.concatenate([foot_send.reshape(n_source, cap * TILE), meta_send, meta_pad], axis=1)
    recv = lax.all_to_all(send, "cell", split_axis=0, concat_axis=0, tiled=True)

    my_group = lax.axis_index("tm")
    groups = lax.axis_size("tm")
    copies = jnp.broadcast_to(flux[None], (groups,) + flux.shape)
    flux_all = lax.all_to_all(copies, "tm", split_axis=0, concat_axis=0, tiled=True)
    flux_all = flux_all.reshape(groups * slices, directions, cell_count).astype(f32)

    foot_r = recv[:, : cap * TILE].reshape(n_slot, TILE)
    meta_r = recv[:, cap * TILE : cap * TILE + cap].reshape(n_slot).astype(jnp.int32)
    meta_hot = (meta_r[:, None] == jnp.arange(n_meta, dtype=jnp.int32)[None, :]).astype(f32)
    panels = flux.reshape(slices, directions, tiles, TILE).transpose(3, 2, 0, 1)
    panels = panels.reshape(TILE, n_meta * directions)
    every = jnp.dot(foot_r, panels, preferred_element_type=f32).reshape(n_slot, n_meta, directions)
    partial = jnp.sum(every * meta_hot[:, :, None], axis=1)
    flux_all, partial = lax.optimization_barrier((flux_all, partial))
    back = lax.all_to_all(
        partial.reshape(n_source, cap * directions), "cell", split_axis=0, concat_axis=0, tiled=True
    ).reshape(n_slot, directions)

    place_f = place.astype(f32)
    per_block = jnp.dot(place_f.T, back, precision=HI, preferred_element_type=f32)
    partial_value = per_block.reshape(sounds, nb, directions).sum(axis=1)
    stack = jnp.broadcast_to(partial_value[None], (groups,) + partial_value.shape)
    images = lax.all_to_all(stack, "tm", split_axis=0, concat_axis=0, tiled=True).sum(axis=0)
    weighted = obs_weight[:, None] * images
    w_block = jnp.repeat(weighted, nb, axis=0)
    w_send = jnp.dot(place_f, w_block, precision=HI, preferred_element_type=f32)
    w_recv = lax.all_to_all(
        w_send.reshape(n_source, cap * directions), "cell", split_axis=0, concat_axis=0, tiled=True
    ).reshape(n_slot, directions)

    w_meta = (meta_hot[:, :, None] * w_recv[:, None, :]).reshape(n_slot, n_meta * directions)
    adj = jnp.dot(w_meta.T, foot_r.astype(f32), precision=HI, preferred_element_type=f32)
    adj = adj.reshape(tiles, slices, directions, TILE).transpose(1, 2, 0, 3)
    adjoint = adj.reshape(slices, directions, cell_count)

    panel = lax.dynamic_slice(prior, (my_group * slices, 0), (slices, groups * slices))
    coupled = jnp.einsum("ts,skn->tkn", panel, flux_all, precision=HI)
    hess = adjoint + coupled
    return (images, hess)


def solution(mesh):
    in_specs = (
        P("tm", None, "cell"),
        P("cell", "tm", None),
        P("cell", "tm"),
        P("cell", "tm"),
        P("cell", "tm"),
        P("cell", None, None),
        P("cell"),
        P(),
    )
    out_specs = (P("cell", None), P("tm", None, "cell"))
    return jax.shard_map(local, mesh=mesh, in_specs=in_specs, out_specs=out_specs, check_vma=False)
```

```python
import jax
import jax.numpy as jnp
from jax import lax
from jax.sharding import PartitionSpec as P

TILE = 128
HI = lax.Precision.HIGHEST


def local(flux, foot, block_slot, block_time, block_count, request_tiles, obs_weight, prior):
    slices, directions, cell_count = flux.shape
    tiles = cell_count // TILE
    sounds, nb, _ = foot.shape
    n_source = request_tiles.shape[1]
    per_source = request_tiles.shape[2]
    n_blocks = sounds * nb
    cap = 16
    n_slot = n_source * cap
    n_meta = tiles * slices
    f32 = jnp.float32

    live = (jnp.arange(nb, dtype=jnp.int32)[None, :] < block_count).reshape(n_blocks)
    slot_ids = block_slot.reshape(n_blocks)
    source = slot_ids // per_source
    position = slot_ids % per_source
    table = request_tiles[0].reshape(n_source * per_source)
    pick = slot_ids[:, None] == jnp.arange(n_source * per_source, dtype=jnp.int32)[None, :]
    local_tile = jnp.sum(jnp.where(pick, table[None, :], 0), axis=1)
    meta = local_tile * slices + block_time.reshape(n_blocks)
    src_hot = (source[:, None] == jnp.arange(n_source, dtype=jnp.int32)[None, :]) & live[:, None]
    src_hot_b = src_hot.astype(jnp.bfloat16)
    row = jnp.arange(n_blocks, dtype=jnp.int32)
    lower = (row[None, :] < row[:, None]).astype(jnp.bfloat16)
    before = jnp.dot(lower, src_hot_b, preferred_element_type=f32)
    rank = jnp.sum(before * src_hot_b.astype(f32), axis=1).astype(jnp.int32)
    dest = jnp.where(live, source * cap + rank, n_slot)
    place = (dest[None, :] == jnp.arange(n_slot, dtype=jnp.int32)[:, None])
    place_b = place.astype(jnp.bfloat16)
    foot_flat = foot.reshape(n_blocks, TILE)
    foot_send = jnp.dot(place_b, foot_flat, preferred_element_type=f32).astype(jnp.bfloat16)
    meta_send = jnp.dot(place_b, meta.astype(jnp.bfloat16)[:, None], preferred_element_type=f32)
    meta_send = meta_send.reshape(n_source, cap).astype(jnp.bfloat16)
    meta_pad = jnp.zeros((n_source, TILE - cap), jnp.bfloat16)
    send = jnp.concatenate([foot_send.reshape(n_source, cap * TILE), meta_send, meta_pad], axis=1)
    recv = lax.all_to_all(send, "cell", split_axis=0, concat_axis=0, tiled=True)

    my_group = lax.axis_index("tm")
    groups = lax.axis_size("tm")
    shifted = []
    for shift in range(1, groups):
        pairs = [(j, (j + shift) % groups) for j in range(groups)]
        shifted.append(lax.ppermute(flux, "tm", perm=pairs))

    foot_r = recv[:, : cap * TILE].reshape(n_slot, TILE)
    meta_r = recv[:, cap * TILE : cap * TILE + cap].reshape(n_slot).astype(jnp.int32)
    meta_hot = (meta_r[:, None] == jnp.arange(n_meta, dtype=jnp.int32)[None, :]).astype(f32)
    panels = flux.reshape(slices, directions, tiles, TILE).transpose(3, 2, 0, 1)
    panels = panels.reshape(TILE, n_meta * directions)
    every = jnp.dot(foot_r, panels, preferred_element_type=f32).reshape(n_slot, n_meta, directions)
    partial = jnp.sum(every * meta_hot[:, :, None], axis=1)
    back = lax.all_to_all(
        partial.reshape(n_source, cap * directions), "cell", split_axis=0, concat_axis=0, tiled=True
    ).reshape(n_slot, directions)

    place_f = place.astype(f32)
    per_block = jnp.dot(place_f.T, back, precision=HI, preferred_element_type=f32)
    partial_value = per_block.reshape(sounds, nb, directions).sum(axis=1)
    stack = jnp.broadcast_to(partial_value[None], (groups,) + partial_value.shape)
    images = lax.all_to_all(stack, "tm", split_axis=0, concat_axis=0, tiled=True).sum(axis=0)
    weighted = obs_weight[:, None] * images
    w_block = jnp.repeat(weighted, nb, axis=0)
    w_send = jnp.dot(place_f, w_block, precision=HI, preferred_element_type=f32)
    w_recv = lax.all_to_all(
        w_send.reshape(n_source, cap * directions), "cell", split_axis=0, concat_axis=0, tiled=True
    ).reshape(n_slot, directions)

    w_meta = (meta_hot[:, :, None] * w_recv[:, None, :]).reshape(n_slot, n_meta * directions)
    adj = jnp.dot(w_meta.T, foot_r.astype(f32), precision=HI, preferred_element_type=f32)
    adj = adj.reshape(tiles, slices, directions, TILE).transpose(1, 2, 0, 3)
    adjoint = adj.reshape(slices, directions, cell_count)

    rows = lax.dynamic_slice(prior, (my_group * slices, 0), (slices, groups * slices))
    own = lax.dynamic_slice(rows, (0, my_group * slices), (slices, slices))
    coupled = jnp.einsum("ts,skn->tkn", own, flux.astype(f32), precision=HI)
    for shift in range(1, groups):
        origin = (my_group - shift) % groups
        block = lax.dynamic_slice(rows, (0, origin * slices), (slices, slices))
        coupled = coupled + jnp.einsum("ts,skn->tkn", block, shifted[shift - 1].astype(f32), precision=HI)
    hess = adjoint + coupled
    return (images, hess)


def solution(mesh):
    in_specs = (
        P("tm", None, "cell"),
        P("cell", "tm", None),
        P("cell", "tm"),
        P("cell", "tm"),
        P("cell", "tm"),
        P("cell", None, None),
        P("cell"),
        P(),
    )
    out_specs = (P("cell", None), P("tm", None, "cell"))
    return jax.shard_map(local, mesh=mesh, in_specs=in_specs, out_specs=out_specs, check_vma=False)
```

```python
import jax
import jax.numpy as jnp
from jax import lax
from jax.sharding import PartitionSpec as P

TILE = 128
HI = lax.Precision.HIGHEST


def local(flux, foot, block_slot, block_time, block_count, request_tiles, obs_weight, prior):
    slices, directions, cell_count = flux.shape
    tiles = cell_count // TILE
    sounds, nb, _ = foot.shape
    n_source = request_tiles.shape[1]
    per_source = request_tiles.shape[2]
    n_blocks = sounds * nb
    cap = 16
    n_slot = n_source * cap
    n_meta = tiles * slices
    f32 = jnp.float32

    live = (jnp.arange(nb, dtype=jnp.int32)[None, :] < block_count).reshape(n_blocks)
    slot_ids = block_slot.reshape(n_blocks)
    source = slot_ids // per_source
    position = slot_ids % per_source
    table = request_tiles[0].reshape(n_source * per_source)
    pick = slot_ids[:, None] == jnp.arange(n_source * per_source, dtype=jnp.int32)[None, :]
    local_tile = jnp.sum(jnp.where(pick, table[None, :], 0), axis=1)
    meta = local_tile * slices + block_time.reshape(n_blocks)
    src_hot = (source[:, None] == jnp.arange(n_source, dtype=jnp.int32)[None, :]) & live[:, None]
    src_hot_b = src_hot.astype(jnp.bfloat16)
    row = jnp.arange(n_blocks, dtype=jnp.int32)
    lower = (row[None, :] < row[:, None]).astype(jnp.bfloat16)
    before = jnp.dot(lower, src_hot_b, preferred_element_type=f32)
    rank = jnp.sum(before * src_hot_b.astype(f32), axis=1).astype(jnp.int32)
    dest = jnp.where(live, source * cap + rank, n_slot)
    place = (dest[None, :] == jnp.arange(n_slot, dtype=jnp.int32)[:, None])
    place_b = place.astype(jnp.bfloat16)
    foot_flat = foot.reshape(n_blocks, TILE)
    foot_send = jnp.dot(place_b, foot_flat, preferred_element_type=f32).astype(jnp.bfloat16)
    meta_send = jnp.dot(place_b, meta.astype(jnp.bfloat16)[:, None], preferred_element_type=f32)
    meta_send = meta_send.reshape(n_source, cap).astype(jnp.bfloat16)
    meta_pad = jnp.zeros((n_source, TILE - cap), jnp.bfloat16)
    send = jnp.concatenate([foot_send.reshape(n_source, cap * TILE), meta_send, meta_pad], axis=1)
    recv = lax.all_to_all(send, "cell", split_axis=0, concat_axis=0, tiled=True)

    my_group = lax.axis_index("tm")
    groups = lax.axis_size("tm")
    copies = jnp.broadcast_to(flux[None], (groups,) + flux.shape)
    flux_all = lax.all_to_all(copies, "tm", split_axis=0, concat_axis=0, tiled=True)
    flux_all = flux_all.reshape(groups * slices, directions, cell_count).astype(f32)

    foot_r = recv[:, : cap * TILE].reshape(n_slot, TILE)
    meta_r = recv[:, cap * TILE : cap * TILE + cap].reshape(n_slot).astype(jnp.int32)
    meta_hot = (meta_r[:, None] == jnp.arange(n_meta, dtype=jnp.int32)[None, :]).astype(f32)
    panels = flux.reshape(slices, directions, tiles, TILE).transpose(3, 2, 0, 1)
    panels = panels.reshape(TILE, n_meta * directions)
    every = jnp.dot(foot_r, panels, preferred_element_type=f32).reshape(n_slot, n_meta, directions)
    partial = jnp.sum(every * meta_hot[:, :, None], axis=1)
    panel = lax.dynamic_slice(prior, (my_group * slices, 0), (slices, groups * slices))
    coupled = jnp.einsum("ts,skn->tkn", panel, flux_all, precision=HI)
    coupled, partial = lax.optimization_barrier((coupled, partial))
    back = lax.all_to_all(
        partial.reshape(n_source, cap * directions), "cell", split_axis=0, concat_axis=0, tiled=True
    ).reshape(n_slot, directions)

    place_f = place.astype(f32)
    per_block = jnp.dot(place_f.T, back, precision=HI, preferred_element_type=f32)
    partial_value = per_block.reshape(sounds, nb, directions).sum(axis=1)
    stack = jnp.broadcast_to(partial_value[None], (groups,) + partial_value.shape)
    images = lax.all_to_all(stack, "tm", split_axis=0, concat_axis=0, tiled=True).sum(axis=0)
    weighted = obs_weight[:, None] * images
    w_block = jnp.repeat(weighted, nb, axis=0)
    w_send = jnp.dot(place_f, w_block, precision=HI, preferred_element_type=f32)
    w_recv = lax.all_to_all(
        w_send.reshape(n_source, cap * directions), "cell", split_axis=0, concat_axis=0, tiled=True
    ).reshape(n_slot, directions)

    hot_tt = meta_hot.reshape(n_slot, tiles, slices).transpose(0, 2, 1)
    w_meta = (hot_tt[:, :, None, :] * w_recv[:, None, :, None]).reshape(n_slot, n_meta * directions)
    adj = jnp.dot(w_meta.T, foot_r.astype(f32), precision=HI, preferred_element_type=f32)
    adjoint = adj.reshape(slices, directions, cell_count)

    hess = adjoint + coupled
    return (images, hess)


def solution(mesh):
    in_specs = (
        P("tm", None, "cell"),
        P("cell", "tm", None),
        P("cell", "tm"),
        P("cell", "tm"),
        P("cell", "tm"),
        P("cell", None, None),
        P("cell"),
        P(),
    )
    out_specs = (P("cell", None), P("tm", None, "cell"))
    return jax.shard_map(local, mesh=mesh, in_specs=in_specs, out_specs=out_specs, check_vma=False)
```

```python
import jax
import jax.numpy as jnp
from jax import lax
from jax.sharding import PartitionSpec as P

TILE = 128
HI = lax.Precision.HIGHEST


def local(flux, foot, block_slot, block_time, block_count, request_tiles, obs_weight, prior):
    slices, directions, cell_count = flux.shape
    tiles = cell_count // TILE
    sounds, nb, _ = foot.shape
    n_source = request_tiles.shape[1]
    per_source = request_tiles.shape[2]
    n_blocks = sounds * nb
    cap = 16
    n_slot = n_source * cap
    n_meta = tiles * slices
    f32 = jnp.float32

    live = (jnp.arange(nb, dtype=jnp.int32)[None, :] < block_count).reshape(n_blocks)
    slot_ids = block_slot.reshape(n_blocks)
    source = slot_ids // per_source
    position = slot_ids % per_source
    table = request_tiles[0].reshape(n_source * per_source)
    pick = slot_ids[:, None] == jnp.arange(n_source * per_source, dtype=jnp.int32)[None, :]
    local_tile = jnp.sum(jnp.where(pick, table[None, :], 0), axis=1)
    meta = local_tile * slices + block_time.reshape(n_blocks)
    src_hot = (source[:, None] == jnp.arange(n_source, dtype=jnp.int32)[None, :]) & live[:, None]
    src_hot_b = src_hot.astype(jnp.bfloat16)
    row = jnp.arange(n_blocks, dtype=jnp.int32)
    lower = (row[None, :] < row[:, None]).astype(jnp.bfloat16)
    before = jnp.dot(lower, src_hot_b, preferred_element_type=f32)
    rank = jnp.sum(before * src_hot_b.astype(f32), axis=1).astype(jnp.int32)
    dest = jnp.where(live, source * cap + rank, n_slot)
    place = (dest[None, :] == jnp.arange(n_slot, dtype=jnp.int32)[:, None])
    place_b = place.astype(jnp.bfloat16)
    foot_flat = foot.reshape(n_blocks, TILE)
    foot_send = jnp.dot(place_b, foot_flat, preferred_element_type=f32).astype(jnp.bfloat16)
    meta_send = jnp.dot(place_b, meta.astype(jnp.bfloat16)[:, None], preferred_element_type=f32)
    meta_send = meta_send.reshape(n_source, cap).astype(jnp.bfloat16)
    sound_of = (row // nb).astype(jnp.bfloat16)[:, None]
    sound_send = jnp.dot(place_b, sound_of, preferred_element_type=f32)
    sound_send = sound_send.reshape(n_source, cap).astype(jnp.bfloat16)
    meta_pad = jnp.zeros((n_source, TILE - 2 * cap), jnp.bfloat16)
    send = jnp.concatenate(
        [foot_send.reshape(n_source, cap * TILE), meta_send, sound_send, meta_pad], axis=1
    )
    recv = lax.all_to_all(send, "cell", split_axis=0, concat_axis=0, tiled=True)

    my_group = lax.axis_index("tm")
    groups = lax.axis_size("tm")
    copies = jnp.broadcast_to(flux[None], (groups,) + flux.shape)
    flux_all = lax.all_to_all(copies, "tm", split_axis=0, concat_axis=0, tiled=True)
    flux_all = flux_all.reshape(groups * slices, directions, cell_count).astype(f32)

    foot_r = recv[:, : cap * TILE].reshape(n_slot, TILE)
    meta_r = recv[:, cap * TILE : cap * TILE + cap].reshape(n_slot).astype(jnp.int32)
    meta_hot = (meta_r[:, None] == jnp.arange(n_meta, dtype=jnp.int32)[None, :]).astype(f32)
    panels = flux.reshape(slices, directions, tiles, TILE).transpose(3, 2, 0, 1)
    panels = panels.reshape(TILE, n_meta * directions)
    every = jnp.dot(foot_r, panels, preferred_element_type=f32).reshape(n_slot, n_meta, directions)
    partial = jnp.sum(every * meta_hot[:, :, None], axis=1)
    panel = lax.dynamic_slice(prior, (my_group * slices, 0), (slices, groups * slices))
    coupled = jnp.einsum("ts,skn->tkn", panel, flux_all, precision=HI)
    coupled, partial = lax.optimization_barrier((coupled, partial))
    sound_r = recv[:, cap * TILE + cap : cap * TILE + 2 * cap].astype(jnp.int32)
    sound_hot = (sound_r[:, None, :] == jnp.arange(sounds, dtype=jnp.int32)[None, :, None]).astype(f32)
    share = jnp.einsum(
        "dsr,drk->dsk", sound_hot, partial.reshape(n_source, cap, directions), precision=HI
    )

    my_cell = lax.axis_index("cell")
    own_weight = jnp.where(my_group == 0, obs_weight, jnp.zeros_like(obs_weight))
    weight_share = lax.dynamic_update_slice(
        jnp.zeros((n_source, sounds), f32), own_weight[None, :], (my_cell, 0)
    )
    total = jnp.concatenate(
        [share.reshape(-1, TILE), weight_share.reshape(-1, TILE)], axis=0
    )
    total = lax.psum(total, ("cell", "tm"))
    split = n_source * sounds * directions // TILE
    obs_all = total[:split].reshape(n_source, sounds, directions)
    weight_all = total[split:].reshape(n_source, sounds)
    images = lax.dynamic_index_in_dim(obs_all, my_cell, axis=0, keepdims=False)
    weighted_all = weight_all[:, :, None] * obs_all
    w_recv = jnp.einsum("dsr,dsk->drk", sound_hot, weighted_all, precision=HI)
    w_recv = w_recv.reshape(n_slot, directions)

    hot_tt = meta_hot.reshape(n_slot, tiles, slices).transpose(0, 2, 1)
    w_meta = (hot_tt[:, :, None, :] * w_recv[:, None, :, None]).reshape(n_slot, n_meta * directions)
    adj = jnp.dot(w_meta.T, foot_r.astype(f32), precision=HI, preferred_element_type=f32)
    adjoint = adj.reshape(slices, directions, cell_count)

    hess = adjoint + coupled
    return (images, hess)


def solution(mesh):
    in_specs = (
        P("tm", None, "cell"),
        P("cell", "tm", None),
        P("cell", "tm"),
        P("cell", "tm"),
        P("cell", "tm"),
        P("cell", None, None),
        P("cell"),
        P(),
    )
    out_specs = (P("cell", None), P("tm", None, "cell"))
    return jax.shard_map(local, mesh=mesh, in_specs=in_specs, out_specs=out_specs, check_vma=False)
```

```python
import jax
import jax.numpy as jnp
from jax import lax
from jax.sharding import Mesh, PartitionSpec as P

TILE = 128
HI = lax.Precision.HIGHEST


def cell_exchange(x):
    rows = x.shape[0]
    side = lax.axis_size("cz")
    x = x.reshape((side, rows // side) + x.shape[1:])
    x = lax.all_to_all(x, "cy", split_axis=1, concat_axis=1, tiled=True)
    x = lax.all_to_all(x, "cz", split_axis=0, concat_axis=0, tiled=True)
    return x.reshape((rows,) + x.shape[2:])


def local(flux, foot, block_slot, block_time, block_count, request_tiles, obs_weight, prior):
    slices, directions, cell_count = flux.shape
    tiles = cell_count // TILE
    sounds, nb, _ = foot.shape
    n_source = request_tiles.shape[1]
    per_source = request_tiles.shape[2]
    n_blocks = sounds * nb
    cap = 16
    n_slot = n_source * cap
    n_meta = tiles * slices
    f32 = jnp.float32

    live = (jnp.arange(nb, dtype=jnp.int32)[None, :] < block_count).reshape(n_blocks)
    slot_ids = block_slot.reshape(n_blocks)
    source = slot_ids // per_source
    position = slot_ids % per_source
    table = request_tiles[0].reshape(n_source * per_source)
    pick = slot_ids[:, None] == jnp.arange(n_source * per_source, dtype=jnp.int32)[None, :]
    local_tile = jnp.sum(jnp.where(pick, table[None, :], 0), axis=1)
    meta = local_tile * slices + block_time.reshape(n_blocks)
    src_hot = (source[:, None] == jnp.arange(n_source, dtype=jnp.int32)[None, :]) & live[:, None]
    src_hot_b = src_hot.astype(jnp.bfloat16)
    row = jnp.arange(n_blocks, dtype=jnp.int32)
    lower = (row[None, :] < row[:, None]).astype(jnp.bfloat16)
    before = jnp.dot(lower, src_hot_b, preferred_element_type=f32)
    rank = jnp.sum(before * src_hot_b.astype(f32), axis=1).astype(jnp.int32)
    dest = jnp.where(live, source * cap + rank, n_slot)
    place = (dest[None, :] == jnp.arange(n_slot, dtype=jnp.int32)[:, None])
    place_b = place.astype(jnp.bfloat16)
    foot_flat = foot.reshape(n_blocks, TILE)
    foot_send = jnp.dot(place_b, foot_flat, preferred_element_type=f32).astype(jnp.bfloat16)
    meta_send = jnp.dot(place_b, meta.astype(jnp.bfloat16)[:, None], preferred_element_type=f32)
    meta_send = meta_send.reshape(n_source, cap).astype(jnp.bfloat16)
    meta_pad = jnp.zeros((n_source, TILE - cap), jnp.bfloat16)
    send = jnp.concatenate([foot_send.reshape(n_source, cap * TILE), meta_send, meta_pad], axis=1)
    recv = cell_exchange(send)

    my_group = lax.axis_index("tm")
    groups = lax.axis_size("tm")
    copies = jnp.broadcast_to(flux[None], (groups,) + flux.shape)
    flux_all = lax.all_to_all(copies, "tm", split_axis=0, concat_axis=0, tiled=True)
    flux_all = flux_all.reshape(groups * slices, directions, cell_count).astype(f32)

    foot_r = recv[:, : cap * TILE].reshape(n_slot, TILE)
    meta_r = recv[:, cap * TILE : cap * TILE + cap].reshape(n_slot).astype(jnp.int32)
    meta_hot = (meta_r[:, None] == jnp.arange(n_meta, dtype=jnp.int32)[None, :]).astype(f32)
    panels = flux.reshape(slices, directions, tiles, TILE).transpose(3, 2, 0, 1)
    panels = panels.reshape(TILE, n_meta * directions)
    every = jnp.dot(foot_r, panels, preferred_element_type=f32).reshape(n_slot, n_meta, directions)
    partial = jnp.sum(every * meta_hot[:, :, None], axis=1)
    panel = lax.dynamic_slice(prior, (my_group * slices, 0), (slices, groups * slices))
    coupled = jnp.einsum("ts,skn->tkn", panel, flux_all, precision=HI)
    coupled, partial = lax.optimization_barrier((coupled, partial))
    back = cell_exchange(partial.reshape(n_source, cap * directions)).reshape(n_slot, directions)

    place_f = place.astype(f32)
    per_block = jnp.dot(place_f.T, back, precision=HI, preferred_element_type=f32)
    partial_value = per_block.reshape(sounds, nb, directions).sum(axis=1)
    stack = jnp.broadcast_to(partial_value[None], (groups,) + partial_value.shape)
    images = lax.all_to_all(stack, "tm", split_axis=0, concat_axis=0, tiled=True).sum(axis=0)
    weighted = obs_weight[:, None] * images
    w_block = jnp.repeat(weighted, nb, axis=0)
    w_send = jnp.dot(place_f, w_block, precision=HI, preferred_element_type=f32)
    w_recv = cell_exchange(w_send.reshape(n_source, cap * directions)).reshape(n_slot, directions)

    hot_tt = meta_hot.reshape(n_slot, tiles, slices).transpose(0, 2, 1)
    w_meta = (hot_tt[:, :, None, :] * w_recv[:, None, :, None]).reshape(n_slot, n_meta * directions)
    adj = jnp.dot(w_meta.T, foot_r.astype(f32), precision=HI, preferred_element_type=f32)
    adjoint = adj.reshape(slices, directions, cell_count)

    hess = adjoint + coupled
    return (images, hess)


def solution(mesh):
    n_cell, n_tm = mesh.devices.shape
    cz = int(round(n_cell ** 0.5))
    grid = Mesh(mesh.devices.reshape(cz, n_cell // cz, n_tm), ("cz", "cy", "tm"))
    cell = ("cz", "cy")
    in_specs = (
        P("tm", None, cell),
        P(cell, "tm", None),
        P(cell, "tm"),
        P(cell, "tm"),
        P(cell, "tm"),
        P(cell, None, None),
        P(cell),
        P(),
    )
    out_specs = (P(cell, None), P("tm", None, cell))
    return jax.shard_map(local, mesh=grid, in_specs=in_specs, out_specs=out_specs, check_vma=False)
```

```python
import jax
import jax.numpy as jnp
from jax import lax
from jax.sharding import PartitionSpec as P

TILE = 128
HI = lax.Precision.HIGHEST


def local(flux, foot, block_slot, block_time, block_count, request_tiles, obs_weight, prior):
    slices, directions, cell_count = flux.shape
    tiles = cell_count // TILE
    sounds, nb, _ = foot.shape
    n_source = request_tiles.shape[1]
    per_source = request_tiles.shape[2]
    n_blocks = sounds * nb
    cap = 16
    n_slot = n_source * cap
    n_meta = tiles * slices
    f32 = jnp.float32

    live = (jnp.arange(nb, dtype=jnp.int32)[None, :] < block_count).reshape(n_blocks)
    slot_ids = block_slot.reshape(n_blocks)
    source = slot_ids // per_source
    position = slot_ids % per_source
    table = request_tiles[0].reshape(n_source * per_source)
    pick = slot_ids[:, None] == jnp.arange(n_source * per_source, dtype=jnp.int32)[None, :]
    local_tile = jnp.sum(jnp.where(pick, table[None, :], 0), axis=1)
    meta = local_tile * slices + block_time.reshape(n_blocks)
    src_hot = (source[:, None] == jnp.arange(n_source, dtype=jnp.int32)[None, :]) & live[:, None]
    src_hot_b = src_hot.astype(jnp.bfloat16)
    row = jnp.arange(n_blocks, dtype=jnp.int32)
    lower = (row[None, :] < row[:, None]).astype(jnp.bfloat16)
    before = jnp.dot(lower, src_hot_b, preferred_element_type=f32)
    rank = jnp.sum(before * src_hot_b.astype(f32), axis=1).astype(jnp.int32)
    dest = jnp.where(live, source * cap + rank, n_slot)
    place = (dest[None, :] == jnp.arange(n_slot, dtype=jnp.int32)[:, None])
    place_b = place.astype(jnp.bfloat16)
    foot_flat = foot.reshape(n_blocks, TILE)
    foot_send = jnp.dot(place_b, foot_flat, preferred_element_type=f32).astype(jnp.bfloat16)
    meta_send = jnp.dot(place_b, meta.astype(jnp.bfloat16)[:, None], preferred_element_type=f32)
    meta_send = meta_send.reshape(n_source, cap).astype(jnp.bfloat16)
    meta_pad = jnp.zeros((n_source, TILE - cap), jnp.bfloat16)
    send = jnp.concatenate([foot_send.reshape(n_source, cap * TILE), meta_send, meta_pad], axis=1)
    recv = lax.all_to_all(send, "cell", split_axis=0, concat_axis=0, tiled=True)

    my_group = lax.axis_index("tm")
    groups = lax.axis_size("tm")
    copies = jnp.broadcast_to(flux[None], (groups,) + flux.shape)
    flux_all = lax.all_to_all(copies, "tm", split_axis=0, concat_axis=0, tiled=True)
    flux_all = flux_all.reshape(groups * slices, directions, cell_count).astype(f32)

    foot_r = recv[:, : cap * TILE].reshape(n_slot, TILE)
    meta_r = recv[:, cap * TILE : cap * TILE + cap].reshape(n_slot).astype(jnp.int32)
    meta_hot = (meta_r[:, None] == jnp.arange(n_meta, dtype=jnp.int32)[None, :]).astype(f32)
    panels = flux.reshape(slices, directions, tiles, TILE).transpose(3, 2, 0, 1)
    panels = panels.reshape(TILE, n_meta * directions)
    every = jnp.dot(foot_r, panels, preferred_element_type=f32).reshape(n_slot, n_meta, directions)
    partial = jnp.sum(every * meta_hot[:, :, None], axis=1)
    panel = lax.dynamic_slice(prior, (my_group * slices, 0), (slices, groups * slices))
    coupled = jnp.einsum("ts,skn->tkn", panel, flux_all, precision=HI)
    place_f = place.astype(f32)
    foot_w = foot_r.astype(f32)
    keep = (coupled, meta_hot, foot_w, place_f)
    partial, keep = lax.optimization_barrier((partial, keep))
    back = lax.all_to_all(
        partial.reshape(n_source, cap * directions), "cell", split_axis=0, concat_axis=0, tiled=True
    ).reshape(n_slot, directions)
    back, keep = lax.optimization_barrier((back, keep))
    coupled, meta_hot, foot_w, place_f = keep

    per_block = jnp.dot(place_f.T, back, precision=HI, preferred_element_type=f32)
    partial_value = per_block.reshape(sounds, nb, directions).sum(axis=1)
    stack = jnp.broadcast_to(partial_value[None], (groups,) + partial_value.shape)
    keep = (coupled, meta_hot, foot_w, place_f)
    stack, keep = lax.optimization_barrier((stack, keep))
    gathered = lax.all_to_all(stack, "tm", split_axis=0, concat_axis=0, tiled=True)
    gathered, keep = lax.optimization_barrier((gathered, keep))
    coupled, meta_hot, foot_w, place_f = keep
    images = gathered.sum(axis=0)
    weighted = obs_weight[:, None] * images
    w_block = jnp.repeat(weighted, nb, axis=0)
    w_send = jnp.dot(place_f, w_block, precision=HI, preferred_element_type=f32)
    hot_tt = meta_hot.reshape(n_slot, tiles, slices).transpose(0, 2, 1)
    keep = (coupled, hot_tt, foot_w)
    w_send, keep = lax.optimization_barrier((w_send, keep))
    w_recv = lax.all_to_all(
        w_send.reshape(n_source, cap * directions), "cell", split_axis=0, concat_axis=0, tiled=True
    ).reshape(n_slot, directions)
    w_recv, keep = lax.optimization_barrier((w_recv, keep))
    coupled, hot_tt, foot_w = keep

    w_meta = (hot_tt[:, :, None, :] * w_recv[:, None, :, None]).reshape(n_slot, n_meta * directions)
    adj = jnp.dot(w_meta.T, foot_w, precision=HI, preferred_element_type=f32)
    adjoint = adj.reshape(slices, directions, cell_count)

    hess = adjoint + coupled
    return (images, hess)


def solution(mesh):
    in_specs = (
        P("tm", None, "cell"),
        P("cell", "tm", None),
        P("cell", "tm"),
        P("cell", "tm"),
        P("cell", "tm"),
        P("cell", None, None),
        P("cell"),
        P(),
    )
    out_specs = (P("cell", None), P("tm", None, "cell"))
    return jax.shard_map(local, mesh=mesh, in_specs=in_specs, out_specs=out_specs, check_vma=False)
```

```python
import jax
import jax.numpy as jnp
from jax import lax
from jax.sharding import PartitionSpec as P

TILE = 128
HI = lax.Precision.HIGHEST


def local(flux, foot, block_slot, block_time, block_count, request_tiles, obs_weight, prior):
    slices, directions, cell_count = flux.shape
    tiles = cell_count // TILE
    sounds, nb, _ = foot.shape
    n_source = request_tiles.shape[1]
    per_source = request_tiles.shape[2]
    n_blocks = sounds * nb
    cap = 16
    n_slot = n_source * cap
    n_meta = tiles * slices
    f32 = jnp.float32

    live = (jnp.arange(nb, dtype=jnp.int32)[None, :] < block_count).reshape(n_blocks)
    slot_ids = block_slot.reshape(n_blocks)
    source = slot_ids // per_source
    position = slot_ids % per_source
    table = request_tiles[0].reshape(n_source * per_source)
    pick = slot_ids[:, None] == jnp.arange(n_source * per_source, dtype=jnp.int32)[None, :]
    local_tile = jnp.sum(jnp.where(pick, table[None, :], 0), axis=1)
    meta = local_tile * slices + block_time.reshape(n_blocks)
    src_hot = (source[:, None] == jnp.arange(n_source, dtype=jnp.int32)[None, :]) & live[:, None]
    src_hot_b = src_hot.astype(jnp.bfloat16)
    row = jnp.arange(n_blocks, dtype=jnp.int32)
    lower = (row[None, :] < row[:, None]).astype(jnp.bfloat16)
    before = jnp.dot(lower, src_hot_b, preferred_element_type=f32)
    rank = jnp.sum(before * src_hot_b.astype(f32), axis=1).astype(jnp.int32)
    dest = jnp.where(live, source * cap + rank, n_slot)
    place = (dest[None, :] == jnp.arange(n_slot, dtype=jnp.int32)[:, None])
    place_b = place.astype(jnp.bfloat16)
    foot_flat = foot.reshape(n_blocks, TILE)
    foot_send = jnp.dot(place_b, foot_flat, preferred_element_type=f32).astype(jnp.bfloat16)
    meta_send = jnp.dot(place_b, meta.astype(jnp.bfloat16)[:, None], preferred_element_type=f32)
    meta_send = meta_send.reshape(n_source, cap).astype(jnp.bfloat16)
    meta_pad = jnp.zeros((n_source, TILE - cap), jnp.bfloat16)
    send = jnp.concatenate([foot_send.reshape(n_source, cap * TILE), meta_send, meta_pad], axis=1)
    recv = lax.all_to_all(send, "cell", split_axis=0, concat_axis=0, tiled=True)

    my_group = lax.axis_index("tm")
    groups = lax.axis_size("tm")
    copies = jnp.broadcast_to(flux[None], (groups,) + flux.shape)
    flux_all = lax.all_to_all(copies, "tm", split_axis=0, concat_axis=0, tiled=True)
    flux_all = flux_all.reshape(groups * slices, directions, cell_count).astype(f32)

    foot_r = recv[:, : cap * TILE].reshape(n_slot, TILE)
    meta_r = recv[:, cap * TILE : cap * TILE + cap].reshape(n_slot).astype(jnp.int32)
    meta_hot = (meta_r[:, None] == jnp.arange(n_meta, dtype=jnp.int32)[None, :]).astype(f32)
    panels = flux.reshape(slices, directions, tiles, TILE).transpose(3, 2, 0, 1)
    panels = panels.reshape(TILE, n_meta * directions)
    every = jnp.dot(foot_r, panels, preferred_element_type=f32).reshape(n_slot, n_meta, directions)
    partial = jnp.sum(every * meta_hot[:, :, None], axis=1)
    panel = lax.dynamic_slice(prior, (my_group * slices, 0), (slices, groups * slices))
    coupled = jnp.einsum("ts,skn->tkn", panel, flux_all, precision=HI)
    coupled, partial = lax.optimization_barrier((coupled, partial))
    back = lax.all_to_all(
        partial.reshape(n_source, cap * directions), "cell", split_axis=0, concat_axis=0, tiled=True
    ).reshape(n_slot, directions)

    place_f = place.astype(f32)
    of_sound = (row[:, None] // nb == jnp.arange(sounds, dtype=jnp.int32)[None, :]).astype(f32)
    gather_sound = jnp.dot(of_sound.T, place_f.T, precision=HI, preferred_element_type=f32)
    slot_weight = jnp.dot(place_f, of_sound * obs_weight[None, :], precision=HI, preferred_element_type=f32)
    slot_weight = jnp.tile(slot_weight, (1, groups))
    partial_value = jnp.dot(gather_sound, back, precision=HI, preferred_element_type=f32)
    stack = jnp.broadcast_to(partial_value[None], (groups,) + partial_value.shape)
    gathered = lax.all_to_all(stack, "tm", split_axis=0, concat_axis=0, tiled=True)
    images = gathered.sum(axis=0)
    gathered = gathered.reshape(groups * sounds, directions)
    w_send = jnp.dot(slot_weight, gathered, precision=HI, preferred_element_type=f32)
    w_recv = lax.all_to_all(
        w_send.reshape(n_source, cap * directions), "cell", split_axis=0, concat_axis=0, tiled=True
    ).reshape(n_slot, directions)

    tile_r = meta_r // slices
    time_r = meta_r % slices
    hot_time = (time_r[:, None] == jnp.arange(slices, dtype=jnp.int32)[None, :]).astype(f32)
    hot_tile = (tile_r[:, None] == jnp.arange(tiles, dtype=jnp.int32)[None, :]).astype(f32)
    foot_tiles = (hot_tile[:, :, None] * foot_r.astype(f32)[:, None, :]).reshape(n_slot, cell_count)
    w_time = (hot_time[:, :, None] * w_recv[:, None, :]).reshape(n_slot, slices * directions)
    adj = jnp.dot(w_time.T, foot_tiles, precision=HI, preferred_element_type=f32)
    adjoint = adj.reshape(slices, directions, cell_count)

    hess = adjoint + coupled
    return (images, hess)


def solution(mesh):
    in_specs = (
        P("tm", None, "cell"),
        P("cell", "tm", None),
        P("cell", "tm"),
        P("cell", "tm"),
        P("cell", "tm"),
        P("cell", None, None),
        P("cell"),
        P(),
    )
    out_specs = (P("cell", None), P("tm", None, "cell"))
    return jax.shard_map(local, mesh=mesh, in_specs=in_specs, out_specs=out_specs, check_vma=False)
```

```python
import jax
import jax.numpy as jnp
from jax import lax
from jax.sharding import PartitionSpec as P

TILE = 128
HI = lax.Precision.HIGHEST


def local(flux, foot, block_slot, block_time, block_count, request_tiles, obs_weight, prior):
    slices, directions, cell_count = flux.shape
    tiles = cell_count // TILE
    sounds, nb, _ = foot.shape
    n_source = request_tiles.shape[1]
    per_source = request_tiles.shape[2]
    n_blocks = sounds * nb
    cap = 16
    n_slot = n_source * cap
    n_meta = tiles * slices
    f32 = jnp.float32

    live = (jnp.arange(nb, dtype=jnp.int32)[None, :] < block_count).reshape(n_blocks)
    slot_ids = block_slot.reshape(n_blocks)
    source = slot_ids // per_source
    position = slot_ids % per_source
    table = request_tiles[0].reshape(n_source * per_source)
    pick = slot_ids[:, None] == jnp.arange(n_source * per_source, dtype=jnp.int32)[None, :]
    local_tile = jnp.sum(jnp.where(pick, table[None, :], 0), axis=1)
    meta = local_tile * slices + block_time.reshape(n_blocks)
    src_hot = (source[:, None] == jnp.arange(n_source, dtype=jnp.int32)[None, :]) & live[:, None]
    src_hot_b = src_hot.astype(jnp.bfloat16)
    row = jnp.arange(n_blocks, dtype=jnp.int32)
    lower = (row[None, :] < row[:, None]).astype(jnp.bfloat16)
    before = jnp.dot(lower, src_hot_b, preferred_element_type=f32)
    rank = jnp.sum(before * src_hot_b.astype(f32), axis=1).astype(jnp.int32)
    dest = jnp.where(live, source * cap + rank, n_slot)
    place = (dest[None, :] == jnp.arange(n_slot, dtype=jnp.int32)[:, None])
    place_b = place.astype(jnp.bfloat16)
    foot_flat = foot.reshape(n_blocks, TILE)
    foot_send = jnp.dot(place_b, foot_flat, preferred_element_type=f32).astype(jnp.bfloat16)
    meta_send = jnp.dot(place_b, meta.astype(jnp.bfloat16)[:, None], preferred_element_type=f32)
    meta_send = meta_send.reshape(n_source, cap).astype(jnp.bfloat16)
    meta_pad = jnp.zeros((n_source, 2 * TILE - cap), jnp.bfloat16)
    send = jnp.concatenate([foot_send.reshape(n_source, cap * TILE), meta_send, meta_pad], axis=1)
    recv = lax.all_to_all(send, "cell", split_axis=0, concat_axis=0, tiled=True)

    my_group = lax.axis_index("tm")
    groups = lax.axis_size("tm")
    copies = jnp.broadcast_to(flux[None], (groups,) + flux.shape)
    flux_all = lax.all_to_all(copies, "tm", split_axis=0, concat_axis=0, tiled=True)
    flux_all = flux_all.reshape(groups * slices, directions, cell_count).astype(f32)

    foot_r = recv[:, : cap * TILE].reshape(n_slot, TILE)
    meta_r = recv[:, cap * TILE : cap * TILE + cap].reshape(n_slot).astype(jnp.int32)
    meta_hot = (meta_r[:, None] == jnp.arange(n_meta, dtype=jnp.int32)[None, :]).astype(f32)
    panels = flux.reshape(slices, directions, tiles, TILE).transpose(3, 2, 0, 1)
    panels = panels.reshape(TILE, n_meta * directions)
    every = jnp.dot(foot_r, panels, preferred_element_type=f32).reshape(n_slot, n_meta, directions)
    partial = jnp.sum(every * meta_hot[:, :, None], axis=1)
    panel = lax.dynamic_slice(prior, (my_group * slices, 0), (slices, groups * slices))
    coupled = jnp.einsum("ts,skn->tkn", panel, flux_all, precision=HI)
    coupled, partial = lax.optimization_barrier((coupled, partial))
    back = lax.all_to_all(
        partial.reshape(n_source, cap * directions), "cell", split_axis=0, concat_axis=0, tiled=True
    ).reshape(n_slot, directions)

    place_f = place.astype(f32)
    per_block = jnp.dot(place_f.T, back, precision=HI, preferred_element_type=f32)
    partial_value = per_block.reshape(sounds, nb, directions).sum(axis=1)
    stack = jnp.broadcast_to(partial_value[None], (groups,) + partial_value.shape)
    images = lax.all_to_all(stack, "tm", split_axis=0, concat_axis=0, tiled=True).sum(axis=0)
    weighted = obs_weight[:, None] * images
    w_block = jnp.repeat(weighted, nb, axis=0)
    w_send = jnp.dot(place_f, w_block, precision=HI, preferred_element_type=f32)
    w_recv = lax.all_to_all(
        w_send.reshape(n_source, cap * directions), "cell", split_axis=0, concat_axis=0, tiled=True
    ).reshape(n_slot, directions)

    hot_tt = meta_hot.reshape(n_slot, tiles, slices).transpose(0, 2, 1)
    w_meta = (hot_tt[:, :, None, :] * w_recv[:, None, :, None]).reshape(n_slot, n_meta * directions)
    adj = jnp.dot(w_meta.T, foot_r.astype(f32), precision=HI, preferred_element_type=f32)
    adjoint = adj.reshape(slices, directions, cell_count)

    hess = adjoint + coupled
    return (images, hess)


def solution(mesh):
    in_specs = (
        P("tm", None, "cell"),
        P("cell", "tm", None),
        P("cell", "tm"),
        P("cell", "tm"),
        P("cell", "tm"),
        P("cell", None, None),
        P("cell"),
        P(),
    )
    out_specs = (P("cell", None), P("tm", None, "cell"))
    return jax.shard_map(local, mesh=mesh, in_specs=in_specs, out_specs=out_specs, check_vma=False)
```

```python
import jax
import jax.numpy as jnp
from jax import lax
from jax.sharding import PartitionSpec as P

TILE = 128
HI = lax.Precision.HIGHEST


def local(flux, foot, block_slot, block_time, block_count, request_tiles, obs_weight, prior):
    slices, directions, cell_count = flux.shape
    tiles = cell_count // TILE
    sounds, nb, _ = foot.shape
    n_source = request_tiles.shape[1]
    per_source = request_tiles.shape[2]
    n_blocks = sounds * nb
    cap = 16
    n_slot = n_source * cap
    n_meta = tiles * slices
    f32 = jnp.float32

    live = (jnp.arange(nb, dtype=jnp.int32)[None, :] < block_count).reshape(n_blocks)
    slot_ids = block_slot.reshape(n_blocks)
    source = slot_ids // per_source
    position = slot_ids % per_source
    table = request_tiles[0].reshape(n_source * per_source)
    pick = slot_ids[:, None] == jnp.arange(n_source * per_source, dtype=jnp.int32)[None, :]
    local_tile = jnp.sum(jnp.where(pick, table[None, :], 0), axis=1)
    meta = local_tile * slices + block_time.reshape(n_blocks)
    src_hot = (source[:, None] == jnp.arange(n_source, dtype=jnp.int32)[None, :]) & live[:, None]
    src_hot_b = src_hot.astype(jnp.bfloat16)
    row = jnp.arange(n_blocks, dtype=jnp.int32)
    lower = (row[None, :] < row[:, None]).astype(jnp.bfloat16)
    before = jnp.dot(lower, src_hot_b, preferred_element_type=f32)
    rank = jnp.sum(before * src_hot_b.astype(f32), axis=1).astype(jnp.int32)
    dest = jnp.where(live, source * cap + rank, n_slot)
    place = (dest[None, :] == jnp.arange(n_slot, dtype=jnp.int32)[:, None])
    place_b = place.astype(jnp.bfloat16)
    foot_flat = foot.reshape(n_blocks, TILE)
    foot_send = jnp.dot(place_b, foot_flat, preferred_element_type=f32).astype(jnp.bfloat16)
    meta_send = jnp.dot(place_b, meta.astype(jnp.bfloat16)[:, None], preferred_element_type=f32)
    meta_send = meta_send.reshape(n_source, cap).astype(jnp.bfloat16)
    meta_pad = jnp.zeros((n_source, TILE - cap), jnp.bfloat16)
    send = jnp.concatenate([foot_send.reshape(n_source, cap * TILE), meta_send, meta_pad], axis=1)
    recv = lax.all_to_all(send, "cell", split_axis=0, concat_axis=0, tiled=True)

    my_group = lax.axis_index("tm")
    groups = lax.axis_size("tm")
    flux_all = lax.all_gather(flux, "tm", axis=0, tiled=True).astype(f32)

    foot_r = recv[:, : cap * TILE].reshape(n_slot, TILE)
    meta_r = recv[:, cap * TILE : cap * TILE + cap].reshape(n_slot).astype(jnp.int32)
    meta_hot = (meta_r[:, None] == jnp.arange(n_meta, dtype=jnp.int32)[None, :]).astype(f32)
    panels = flux.reshape(slices, directions, tiles, TILE).transpose(3, 2, 0, 1)
    panels = panels.reshape(TILE, n_meta * directions)
    every = jnp.dot(foot_r, panels, preferred_element_type=f32).reshape(n_slot, n_meta, directions)
    partial = jnp.sum(every * meta_hot[:, :, None], axis=1)
    panel = lax.dynamic_slice(prior, (my_group * slices, 0), (slices, groups * slices))
    coupled = jnp.einsum("ts,skn->tkn", panel, flux_all, precision=HI)
    coupled, partial = lax.optimization_barrier((coupled, partial))
    back = lax.all_to_all(
        partial.reshape(n_source, cap * directions), "cell", split_axis=0, concat_axis=0, tiled=True
    ).reshape(n_slot, directions)

    place_f = place.astype(f32)
    per_block = jnp.dot(place_f.T, back, precision=HI, preferred_element_type=f32)
    partial_value = per_block.reshape(sounds, nb, directions).sum(axis=1)
    stack = jnp.broadcast_to(partial_value[None], (groups,) + partial_value.shape)
    images = lax.all_to_all(stack, "tm", split_axis=0, concat_axis=0, tiled=True).sum(axis=0)
    weighted = obs_weight[:, None] * images
    w_block = jnp.repeat(weighted, nb, axis=0)
    w_send = jnp.dot(place_f, w_block, precision=HI, preferred_element_type=f32)
    w_recv = lax.all_to_all(
        w_send.reshape(n_source, cap * directions), "cell", split_axis=0, concat_axis=0, tiled=True
    ).reshape(n_slot, directions)

    hot_tt = meta_hot.reshape(n_slot, tiles, slices).transpose(0, 2, 1)
    w_meta = (hot_tt[:, :, None, :] * w_recv[:, None, :, None]).reshape(n_slot, n_meta * directions)
    adj = jnp.dot(w_meta.T, foot_r.astype(f32), precision=HI, preferred_element_type=f32)
    adjoint = adj.reshape(slices, directions, cell_count)

    hess = adjoint + coupled
    return (images, hess)


def solution(mesh):
    in_specs = (
        P("tm", None, "cell"),
        P("cell", "tm", None),
        P("cell", "tm"),
        P("cell", "tm"),
        P("cell", "tm"),
        P("cell", None, None),
        P("cell"),
        P(),
    )
    out_specs = (P("cell", None), P("tm", None, "cell"))
    return jax.shard_map(local, mesh=mesh, in_specs=in_specs, out_specs=out_specs, check_vma=False)
```

```python
import jax
import jax.numpy as jnp
from jax import lax
from jax.sharding import PartitionSpec as P

TILE = 128
HI = lax.Precision.HIGHEST


def local(flux, foot, block_slot, block_time, block_count, request_tiles, obs_weight, prior):
    slices, directions, cell_count = flux.shape
    tiles = cell_count // TILE
    sounds, nb, _ = foot.shape
    n_source = request_tiles.shape[1]
    per_source = request_tiles.shape[2]
    n_blocks = sounds * nb
    cap = 16
    n_slot = n_source * cap
    n_meta = tiles * slices
    f32 = jnp.float32

    live = (jnp.arange(nb, dtype=jnp.int32)[None, :] < block_count).reshape(n_blocks)
    slot_ids = block_slot.reshape(n_blocks)
    source = slot_ids // per_source
    position = slot_ids % per_source
    table = request_tiles[0].reshape(n_source * per_source)
    pick = slot_ids[:, None] == jnp.arange(n_source * per_source, dtype=jnp.int32)[None, :]
    local_tile = jnp.sum(jnp.where(pick, table[None, :], 0), axis=1)
    meta = local_tile * slices + block_time.reshape(n_blocks)
    src_hot = (source[:, None] == jnp.arange(n_source, dtype=jnp.int32)[None, :]) & live[:, None]
    src_hot_b = src_hot.astype(jnp.bfloat16)
    row = jnp.arange(n_blocks, dtype=jnp.int32)
    lower = (row[None, :] < row[:, None]).astype(jnp.bfloat16)
    before = jnp.dot(lower, src_hot_b, preferred_element_type=f32)
    rank = jnp.sum(before * src_hot_b.astype(f32), axis=1).astype(jnp.int32)
    dest = jnp.where(live, source * cap + rank, n_slot)
    place = (dest[None, :] == jnp.arange(n_slot, dtype=jnp.int32)[:, None])
    place_b = place.astype(jnp.bfloat16)
    foot_flat = foot.reshape(n_blocks, TILE)
    foot_send = jnp.dot(place_b, foot_flat, preferred_element_type=f32).astype(jnp.bfloat16)
    meta_send = jnp.dot(place_b, meta.astype(jnp.bfloat16)[:, None], preferred_element_type=f32)
    meta_send = meta_send.reshape(n_source, cap).astype(jnp.bfloat16)
    meta_pad = jnp.zeros((n_source, TILE - cap), jnp.bfloat16)
    send = jnp.concatenate([foot_send.reshape(n_source, cap * TILE), meta_send, meta_pad], axis=1)
    recv = lax.all_to_all(send, "cell", split_axis=0, concat_axis=0, tiled=True)

    my_group = lax.axis_index("tm")
    groups = lax.axis_size("tm")

    foot_r = recv[:, : cap * TILE].reshape(n_slot, TILE)
    meta_r = recv[:, cap * TILE : cap * TILE + cap].reshape(n_slot).astype(jnp.int32)
    meta_hot = (meta_r[:, None] == jnp.arange(n_meta, dtype=jnp.int32)[None, :]).astype(f32)
    panels = flux.reshape(slices, directions, tiles, TILE).transpose(3, 2, 0, 1)
    panels = panels.reshape(TILE, n_meta * directions)
    every = jnp.dot(foot_r, panels, preferred_element_type=f32).reshape(n_slot, n_meta, directions)
    partial = jnp.sum(every * meta_hot[:, :, None], axis=1)
    flux_late, partial = lax.optimization_barrier((flux, partial))
    back = lax.all_to_all(
        partial.reshape(n_source, cap * directions), "cell", split_axis=0, concat_axis=0, tiled=True
    ).reshape(n_slot, directions)

    place_f = place.astype(f32)
    per_block = jnp.dot(place_f.T, back, precision=HI, preferred_element_type=f32)
    partial_value = per_block.reshape(sounds, nb, directions).sum(axis=1)
    stack = jnp.broadcast_to(partial_value[None], (groups,) + partial_value.shape)
    images = lax.all_to_all(stack, "tm", split_axis=0, concat_axis=0, tiled=True).sum(axis=0)
    weighted = obs_weight[:, None] * images
    w_block = jnp.repeat(weighted, nb, axis=0)
    w_send = jnp.dot(place_f, w_block, precision=HI, preferred_element_type=f32)
    flux_all = lax.all_gather(flux_late, "tm", axis=0, tiled=True).astype(f32)
    panel = lax.dynamic_slice(prior, (my_group * slices, 0), (slices, groups * slices))
    coupled = jnp.einsum("ts,skn->tkn", panel, flux_all, precision=HI)
    coupled, w_send = lax.optimization_barrier((coupled, w_send))
    w_recv = lax.all_to_all(
        w_send.reshape(n_source, cap * directions), "cell", split_axis=0, concat_axis=0, tiled=True
    ).reshape(n_slot, directions)

    hot_tt = meta_hot.reshape(n_slot, tiles, slices).transpose(0, 2, 1)
    w_meta = (hot_tt[:, :, None, :] * w_recv[:, None, :, None]).reshape(n_slot, n_meta * directions)
    adj = jnp.dot(w_meta.T, foot_r.astype(f32), precision=HI, preferred_element_type=f32)
    adjoint = adj.reshape(slices, directions, cell_count)

    hess = adjoint + coupled
    return (images, hess)


def solution(mesh):
    in_specs = (
        P("tm", None, "cell"),
        P("cell", "tm", None),
        P("cell", "tm"),
        P("cell", "tm"),
        P("cell", "tm"),
        P("cell", None, None),
        P("cell"),
        P(),
    )
    out_specs = (P("cell", None), P("tm", None, "cell"))
    return jax.shard_map(local, mesh=mesh, in_specs=in_specs, out_specs=out_specs, check_vma=False)
```

```python
import jax
import jax.numpy as jnp
from jax import lax
from jax.sharding import PartitionSpec as P

TILE = 128
HI = lax.Precision.HIGHEST


def local(flux, foot, block_slot, block_time, block_count, request_tiles, obs_weight, prior):
    slices, directions, cell_count = flux.shape
    tiles = cell_count // TILE
    sounds, nb, _ = foot.shape
    n_source = request_tiles.shape[1]
    per_source = request_tiles.shape[2]
    n_blocks = sounds * nb
    cap = 16
    n_slot = n_source * cap
    n_meta = tiles * slices
    f32 = jnp.float32

    live = (jnp.arange(nb, dtype=jnp.int32)[None, :] < block_count).reshape(n_blocks)
    slot_ids = block_slot.reshape(n_blocks)
    source = slot_ids // per_source
    position = slot_ids % per_source
    table = request_tiles[0].reshape(n_source * per_source)
    pick = slot_ids[:, None] == jnp.arange(n_source * per_source, dtype=jnp.int32)[None, :]
    local_tile = jnp.sum(jnp.where(pick, table[None, :], 0), axis=1)
    meta = local_tile * slices + block_time.reshape(n_blocks)
    src_hot = (source[:, None] == jnp.arange(n_source, dtype=jnp.int32)[None, :]) & live[:, None]
    src_hot_b = src_hot.astype(jnp.bfloat16)
    row = jnp.arange(n_blocks, dtype=jnp.int32)
    lower = (row[None, :] < row[:, None]).astype(jnp.bfloat16)
    before = jnp.dot(lower, src_hot_b, preferred_element_type=f32)
    rank = jnp.sum(before * src_hot_b.astype(f32), axis=1).astype(jnp.int32)
    dest = jnp.where(live, source * cap + rank, n_slot)
    place = (dest[None, :] == jnp.arange(n_slot, dtype=jnp.int32)[:, None])
    place_b = place.astype(jnp.bfloat16)
    foot_flat = foot.reshape(n_blocks, TILE)
    foot_send = jnp.dot(place_b, foot_flat, preferred_element_type=f32).astype(jnp.bfloat16)
    meta_send = jnp.dot(place_b, meta.astype(jnp.bfloat16)[:, None], preferred_element_type=f32)
    meta_send = meta_send.reshape(n_source, cap).astype(jnp.bfloat16)
    meta_pad = jnp.zeros((n_source, TILE - cap), jnp.bfloat16)
    send = jnp.concatenate([foot_send.reshape(n_source, cap * TILE), meta_send, meta_pad], axis=1)
    recv = lax.all_to_all(send, "cell", split_axis=0, concat_axis=0, tiled=True)

    my_group = lax.axis_index("tm")
    groups = lax.axis_size("tm")

    foot_r = recv[:, : cap * TILE].reshape(n_slot, TILE)
    meta_r = recv[:, cap * TILE : cap * TILE + cap].reshape(n_slot).astype(jnp.int32)
    meta_hot = (meta_r[:, None] == jnp.arange(n_meta, dtype=jnp.int32)[None, :]).astype(f32)
    panels = flux.reshape(slices, directions, tiles, TILE).transpose(3, 2, 0, 1)
    panels = panels.reshape(TILE, n_meta * directions)
    every = jnp.dot(foot_r, panels, preferred_element_type=f32).reshape(n_slot, n_meta, directions)
    partial = jnp.sum(every * meta_hot[:, :, None], axis=1)
    half = directions // 2
    flux_a, partial = lax.optimization_barrier((flux[:, :half], partial))
    back = lax.all_to_all(
        partial.reshape(n_source, cap * directions), "cell", split_axis=0, concat_axis=0, tiled=True
    ).reshape(n_slot, directions)

    place_f = place.astype(f32)
    per_block = jnp.dot(place_f.T, back, precision=HI, preferred_element_type=f32)
    partial_value = per_block.reshape(sounds, nb, directions).sum(axis=1)
    stack = jnp.broadcast_to(partial_value[None], (groups,) + partial_value.shape)
    images = lax.all_to_all(stack, "tm", split_axis=0, concat_axis=0, tiled=True).sum(axis=0)
    weighted = obs_weight[:, None] * images
    w_block = jnp.repeat(weighted, nb, axis=0)
    w_send = jnp.dot(place_f, w_block, precision=HI, preferred_element_type=f32)
    panel = lax.dynamic_slice(prior, (my_group * slices, 0), (slices, groups * slices))
    gathered_a = lax.all_gather(flux_a, "tm", axis=0, tiled=True).astype(f32)
    coupled_a = jnp.einsum("ts,skn->tkn", panel, gathered_a, precision=HI)
    coupled_a, flux_b, w_send = lax.optimization_barrier((coupled_a, flux[:, half:], w_send))
    w_recv = lax.all_to_all(
        w_send.reshape(n_source, cap * directions), "cell", split_axis=0, concat_axis=0, tiled=True
    ).reshape(n_slot, directions)

    hot_tt = meta_hot.reshape(n_slot, tiles, slices).transpose(0, 2, 1)
    w_meta = (hot_tt[:, :, None, :] * w_recv[:, None, :, None]).reshape(n_slot, n_meta * directions)
    adj = jnp.dot(w_meta.T, foot_r.astype(f32), precision=HI, preferred_element_type=f32)
    adjoint = adj.reshape(slices, directions, cell_count)

    gathered_b = lax.all_gather(flux_b, "tm", axis=0, tiled=True).astype(f32)
    coupled_b = jnp.einsum("ts,skn->tkn", panel, gathered_b, precision=HI)
    hess = adjoint + jnp.concatenate([coupled_a, coupled_b], axis=1)
    return (images, hess)


def solution(mesh):
    in_specs = (
        P("tm", None, "cell"),
        P("cell", "tm", None),
        P("cell", "tm"),
        P("cell", "tm"),
        P("cell", "tm"),
        P("cell", None, None),
        P("cell"),
        P(),
    )
    out_specs = (P("cell", None), P("tm", None, "cell"))
    return jax.shard_map(local, mesh=mesh, in_specs=in_specs, out_specs=out_specs, check_vma=False)
```

```python
import jax
import jax.numpy as jnp
from jax import lax
from jax.sharding import PartitionSpec as P

TILE = 128
HI = lax.Precision.HIGHEST


def local(flux, foot, block_slot, block_time, block_count, request_tiles, obs_weight, prior):
    slices, directions, cell_count = flux.shape
    tiles = cell_count // TILE
    sounds, nb, _ = foot.shape
    n_source = request_tiles.shape[1]
    per_source = request_tiles.shape[2]
    n_blocks = sounds * nb
    cap = 16
    n_slot = n_source * cap
    n_meta = tiles * slices
    f32 = jnp.float32

    live = (jnp.arange(nb, dtype=jnp.int32)[None, :] < block_count).reshape(n_blocks)
    slot_ids = block_slot.reshape(n_blocks)
    source = slot_ids // per_source
    position = slot_ids % per_source
    table = request_tiles[0].reshape(n_source * per_source)
    pick = slot_ids[:, None] == jnp.arange(n_source * per_source, dtype=jnp.int32)[None, :]
    local_tile = jnp.sum(jnp.where(pick, table[None, :], 0), axis=1)
    meta = local_tile * slices + block_time.reshape(n_blocks)
    src_hot = (source[:, None] == jnp.arange(n_source, dtype=jnp.int32)[None, :]) & live[:, None]
    src_hot_b = src_hot.astype(jnp.bfloat16)
    row = jnp.arange(n_blocks, dtype=jnp.int32)
    lower = (row[None, :] < row[:, None]).astype(jnp.bfloat16)
    before = jnp.dot(lower, src_hot_b, preferred_element_type=f32)
    rank = jnp.sum(before * src_hot_b.astype(f32), axis=1).astype(jnp.int32)
    dest = jnp.where(live, source * cap + rank, n_slot)
    place = (dest[None, :] == jnp.arange(n_slot, dtype=jnp.int32)[:, None])
    place_b = place.astype(jnp.bfloat16)
    foot_flat = foot.reshape(n_blocks, TILE)
    foot_send = jnp.dot(place_b, foot_flat, preferred_element_type=f32).astype(jnp.bfloat16)
    meta_send = jnp.dot(place_b, meta.astype(jnp.bfloat16)[:, None], preferred_element_type=f32)
    meta_send = meta_send.reshape(n_source, cap).astype(jnp.bfloat16)
    meta_pad = jnp.zeros((n_source, TILE - cap), jnp.bfloat16)
    send = jnp.concatenate([foot_send.reshape(n_source, cap * TILE), meta_send, meta_pad], axis=1)
    recv = lax.all_to_all(send, "cell", split_axis=0, concat_axis=0, tiled=True)

    my_group = lax.axis_index("tm")
    groups = lax.axis_size("tm")
    foot_r = recv[:, : cap * TILE].reshape(n_slot, TILE)
    meta_r = recv[:, cap * TILE : cap * TILE + cap].reshape(n_slot).astype(jnp.int32)
    meta_hot = (meta_r[:, None] == jnp.arange(n_meta, dtype=jnp.int32)[None, :]).astype(f32)
    panels = flux.reshape(slices, directions, tiles, TILE).transpose(3, 2, 0, 1)
    panels = panels.reshape(TILE, n_meta * directions)
    every = jnp.dot(foot_r, panels, preferred_element_type=f32).reshape(n_slot, n_meta, directions)
    partial = jnp.sum(every * meta_hot[:, :, None], axis=1)
    back = lax.all_to_all(
        partial.reshape(n_source, cap * directions), "cell", split_axis=0, concat_axis=0, tiled=True
    ).reshape(n_slot, directions)

    place_f = place.astype(f32)
    per_block = jnp.dot(place_f.T, back, precision=HI, preferred_element_type=f32)
    partial_value = per_block.reshape(sounds, nb, directions).sum(axis=1)
    bf = jnp.bfloat16
    hi = lax.reduce_precision(partial_value, exponent_bits=8, mantissa_bits=7)
    rest = partial_value - hi
    mid = lax.reduce_precision(rest, exponent_bits=8, mantissa_bits=7)
    lo = rest - mid
    pieces = jnp.stack([hi, mid, lo]).astype(bf).reshape(-1, TILE)
    flux_rows = flux.reshape(-1, TILE)
    payload = jnp.concatenate([flux_rows, pieces], axis=0)
    copies = jnp.broadcast_to(payload[None], (groups,) + payload.shape)
    arrived = lax.all_to_all(copies, "tm", split_axis=0, concat_axis=0, tiled=True)
    n_rows = flux_rows.shape[0]
    flux_all = arrived[:, :n_rows].reshape(groups * slices, directions, cell_count).astype(f32)
    parts = arrived[:, n_rows:].reshape(groups, 3, sounds, directions).astype(f32)
    values = (parts[:, 0] + parts[:, 1]) + parts[:, 2]
    images = values.sum(axis=0)
    weighted = obs_weight[:, None] * images
    w_block = jnp.repeat(weighted, nb, axis=0)
    w_send = jnp.dot(place_f, w_block, precision=HI, preferred_element_type=f32)
    panel = lax.dynamic_slice(prior, (my_group * slices, 0), (slices, groups * slices))
    coupled = jnp.einsum("ts,skn->tkn", panel, flux_all, precision=HI)
    w_recv = lax.all_to_all(
        w_send.reshape(n_source, cap * directions), "cell", split_axis=0, concat_axis=0, tiled=True
    ).reshape(n_slot, directions)

    hot_tt = meta_hot.reshape(n_slot, tiles, slices).transpose(0, 2, 1)
    w_meta = (hot_tt[:, :, None, :] * w_recv[:, None, :, None]).reshape(n_slot, n_meta * directions)
    adj = jnp.dot(w_meta.T, foot_r.astype(f32), precision=HI, preferred_element_type=f32)
    adjoint = adj.reshape(slices, directions, cell_count)

    hess = adjoint + coupled
    return (images, hess)


def solution(mesh):
    in_specs = (
        P("tm", None, "cell"),
        P("cell", "tm", None),
        P("cell", "tm"),
        P("cell", "tm"),
        P("cell", "tm"),
        P("cell", None, None),
        P("cell"),
        P(),
    )
    out_specs = (P("cell", None), P("tm", None, "cell"))
    return jax.shard_map(local, mesh=mesh, in_specs=in_specs, out_specs=out_specs, check_vma=False)
```

```python
import jax
import jax.numpy as jnp
from jax import lax
from jax.sharding import PartitionSpec as P

TILE = 128
HI = lax.Precision.HIGHEST


def local(flux, foot, block_slot, block_time, block_count, request_tiles, obs_weight, prior):
    slices, directions, cell_count = flux.shape
    tiles = cell_count // TILE
    sounds, nb, _ = foot.shape
    n_source = request_tiles.shape[1]
    per_source = request_tiles.shape[2]
    n_blocks = sounds * nb
    cap = 16
    n_slot = n_source * cap
    n_meta = tiles * slices
    f32 = jnp.float32

    live = (jnp.arange(nb, dtype=jnp.int32)[None, :] < block_count).reshape(n_blocks)
    slot_ids = block_slot.reshape(n_blocks)
    source = slot_ids // per_source
    position = slot_ids % per_source
    table = request_tiles[0].reshape(n_source * per_source)
    pick = slot_ids[:, None] == jnp.arange(n_source * per_source, dtype=jnp.int32)[None, :]
    local_tile = jnp.sum(jnp.where(pick, table[None, :], 0), axis=1)
    meta = local_tile * slices + block_time.reshape(n_blocks)
    src_hot = (source[:, None] == jnp.arange(n_source, dtype=jnp.int32)[None, :]) & live[:, None]
    src_hot_b = src_hot.astype(jnp.bfloat16)
    row = jnp.arange(n_blocks, dtype=jnp.int32)
    lower = (row[None, :] < row[:, None]).astype(jnp.bfloat16)
    before = jnp.dot(lower, src_hot_b, preferred_element_type=f32)
    rank = jnp.sum(before * src_hot_b.astype(f32), axis=1).astype(jnp.int32)
    dest = jnp.where(live, source * cap + rank, n_slot)
    place = (dest[None, :] == jnp.arange(n_slot, dtype=jnp.int32)[:, None])
    place_b = place.astype(jnp.bfloat16)
    foot_flat = foot.reshape(n_blocks, TILE)
    foot_send = jnp.dot(place_b, foot_flat, preferred_element_type=f32).astype(jnp.bfloat16)
    meta_send = jnp.dot(place_b, meta.astype(jnp.bfloat16)[:, None], preferred_element_type=f32)
    meta_send = meta_send.reshape(n_source, cap).astype(jnp.bfloat16)
    meta_pad = jnp.zeros((n_source, TILE - cap), jnp.bfloat16)
    send = jnp.concatenate([foot_send.reshape(n_source, cap * TILE), meta_send, meta_pad], axis=1)
    recv = lax.all_to_all(send, "cell", split_axis=0, concat_axis=0, tiled=True)

    my_group = lax.axis_index("tm")
    groups = lax.axis_size("tm")
    foot_r = recv[:, : cap * TILE].reshape(n_slot, TILE)
    meta_r = recv[:, cap * TILE : cap * TILE + cap].reshape(n_slot).astype(jnp.int32)
    meta_hot = (meta_r[:, None] == jnp.arange(n_meta, dtype=jnp.int32)[None, :]).astype(f32)
    panels = flux.reshape(slices, directions, tiles, TILE).transpose(3, 2, 0, 1)
    panels = panels.reshape(TILE, n_meta * directions)
    every = jnp.dot(foot_r, panels, preferred_element_type=f32).reshape(n_slot, n_meta, directions)
    partial = jnp.sum(every * meta_hot[:, :, None], axis=1)
    back = lax.all_to_all(
        partial.reshape(n_source, cap * directions), "cell", split_axis=0, concat_axis=0, tiled=True
    ).reshape(n_slot, directions)

    place_f = place.astype(f32)
    per_block = jnp.dot(place_f.T, back, precision=HI, preferred_element_type=f32)
    partial_value = per_block.reshape(sounds, nb, directions).sum(axis=1)
    bf = jnp.bfloat16
    hi = lax.reduce_precision(partial_value, exponent_bits=8, mantissa_bits=7)
    rest = partial_value - hi
    mid = lax.reduce_precision(rest, exponent_bits=8, mantissa_bits=7)
    lo = rest - mid
    pieces = jnp.stack([hi, mid, lo]).astype(bf).reshape(-1, TILE)
    flux_rows = flux.reshape(-1, TILE)
    payload = jnp.concatenate([flux_rows, pieces], axis=0)
    copies = jnp.broadcast_to(payload[None], (groups,) + payload.shape)
    arrived = lax.all_to_all(copies, "tm", split_axis=0, concat_axis=0, tiled=True)
    n_rows = flux_rows.shape[0]
    flux_all = arrived[:, :n_rows].reshape(groups * slices, directions, cell_count).astype(f32)
    parts = arrived[:, n_rows:].reshape(groups, 3, sounds, directions).astype(f32)
    values = (parts[:, 0] + parts[:, 1]) + parts[:, 2]
    images = values.sum(axis=0)
    weighted = obs_weight[:, None] * images
    w_block = jnp.repeat(weighted, nb, axis=0)
    w_send = jnp.dot(place_f, w_block, precision=HI, preferred_element_type=f32)
    panel = lax.dynamic_slice(prior, (my_group * slices, 0), (slices, groups * slices))
    coupled = jnp.einsum("ts,skn->tkn", panel, flux_all, precision=HI)
    w_recv = lax.all_to_all(
        w_send.reshape(n_source, cap * directions), "cell", split_axis=0, concat_axis=0, tiled=True
    ).reshape(n_slot, directions)
    coupled, w_recv = lax.optimization_barrier((coupled, w_recv))

    hot_tt = meta_hot.reshape(n_slot, tiles, slices).transpose(0, 2, 1)
    w_meta = (hot_tt[:, :, None, :] * w_recv[:, None, :, None]).reshape(n_slot, n_meta * directions)
    adj = jnp.dot(w_meta.T, foot_r.astype(f32), precision=HI, preferred_element_type=f32)
    adjoint = adj.reshape(slices, directions, cell_count)

    hess = adjoint + coupled
    return (images, hess)


def solution(mesh):
    in_specs = (
        P("tm", None, "cell"),
        P("cell", "tm", None),
        P("cell", "tm"),
        P("cell", "tm"),
        P("cell", "tm"),
        P("cell", None, None),
        P("cell"),
        P(),
    )
    out_specs = (P("cell", None), P("tm", None, "cell"))
    return jax.shard_map(local, mesh=mesh, in_specs=in_specs, out_specs=out_specs, check_vma=False)
```

```python
import jax
import jax.numpy as jnp
from jax import lax
from jax.sharding import PartitionSpec as P

TILE = 128
HI = lax.Precision.HIGHEST


def local(flux, foot, block_slot, block_time, block_count, request_tiles, obs_weight, prior):
    slices, directions, cell_count = flux.shape
    tiles = cell_count // TILE
    sounds, nb, _ = foot.shape
    n_source = request_tiles.shape[1]
    per_source = request_tiles.shape[2]
    n_blocks = sounds * nb
    cap = 16
    n_slot = n_source * cap
    n_meta = tiles * slices
    f32 = jnp.float32

    live = (jnp.arange(nb, dtype=jnp.int32)[None, :] < block_count).reshape(n_blocks)
    slot_ids = block_slot.reshape(n_blocks)
    source = slot_ids // per_source
    position = slot_ids % per_source
    table = request_tiles[0].reshape(n_source * per_source)
    pick = slot_ids[:, None] == jnp.arange(n_source * per_source, dtype=jnp.int32)[None, :]
    local_tile = jnp.sum(jnp.where(pick, table[None, :], 0), axis=1)
    meta = local_tile * slices + block_time.reshape(n_blocks)
    src_hot = (source[:, None] == jnp.arange(n_source, dtype=jnp.int32)[None, :]) & live[:, None]
    src_hot_b = src_hot.astype(jnp.bfloat16)
    row = jnp.arange(n_blocks, dtype=jnp.int32)
    lower = (row[None, :] < row[:, None]).astype(jnp.bfloat16)
    before = jnp.dot(lower, src_hot_b, preferred_element_type=f32)
    rank = jnp.sum(before * src_hot_b.astype(f32), axis=1).astype(jnp.int32)
    dest = jnp.where(live, source * cap + rank, n_slot)
    place = (dest[None, :] == jnp.arange(n_slot, dtype=jnp.int32)[:, None])
    place_b = place.astype(jnp.bfloat16)
    foot_flat = foot.reshape(n_blocks, TILE)
    foot_send = jnp.dot(place_b, foot_flat, preferred_element_type=f32).astype(jnp.bfloat16)
    meta_send = jnp.sum(jnp.where(place, meta[None, :], 0), axis=1)
    meta_send = meta_send.reshape(n_source, cap).astype(jnp.bfloat16)
    meta_pad = jnp.zeros((n_source, TILE - cap), jnp.bfloat16)
    send = jnp.concatenate([foot_send.reshape(n_source, cap * TILE), meta_send, meta_pad], axis=1)
    recv = lax.all_to_all(send, "cell", split_axis=0, concat_axis=0, tiled=True)

    my_group = lax.axis_index("tm")
    groups = lax.axis_size("tm")
    foot_r = recv[:, : cap * TILE].reshape(n_slot, TILE)
    meta_r = recv[:, cap * TILE : cap * TILE + cap].reshape(n_slot).astype(jnp.int32)
    meta_hot = (meta_r[:, None] == jnp.arange(n_meta, dtype=jnp.int32)[None, :]).astype(f32)
    panels = flux.reshape(slices, directions, tiles, TILE).transpose(3, 2, 0, 1)
    panels = panels.reshape(TILE, n_meta * directions)
    every = jnp.dot(foot_r, panels, preferred_element_type=f32).reshape(n_slot, n_meta, directions)
    partial = jnp.sum(every * meta_hot[:, :, None], axis=1)
    back = lax.all_to_all(
        partial.reshape(n_source, cap * directions), "cell", split_axis=0, concat_axis=0, tiled=True
    ).reshape(n_slot, directions)

    place_f = place.astype(f32)
    per_block = jnp.dot(place_f.T, back, precision=HI, preferred_element_type=f32)
    partial_value = per_block.reshape(sounds, nb, directions).sum(axis=1)
    bf = jnp.bfloat16
    hi = lax.reduce_precision(partial_value, exponent_bits=8, mantissa_bits=7)
    rest = partial_value - hi
    mid = lax.reduce_precision(rest, exponent_bits=8, mantissa_bits=7)
    lo = rest - mid
    pieces = jnp.stack([hi, mid, lo]).astype(bf).reshape(-1, TILE)
    flux_rows = flux.reshape(-1, TILE)
    payload = jnp.concatenate([flux_rows, pieces], axis=0)
    copies = jnp.broadcast_to(payload[None], (groups,) + payload.shape)
    arrived = lax.all_to_all(copies, "tm", split_axis=0, concat_axis=0, tiled=True)
    n_rows = flux_rows.shape[0]
    flux_all = arrived[:, :n_rows].reshape(groups * slices, directions, cell_count).astype(f32)
    parts = arrived[:, n_rows:].reshape(groups, 3, sounds, directions).astype(f32)
    values = (parts[:, 0] + parts[:, 1]) + parts[:, 2]
    images = values.sum(axis=0)
    weighted = obs_weight[:, None] * images
    w_block = jnp.repeat(weighted, nb, axis=0)
    w_send = jnp.dot(place_f, w_block, precision=HI, preferred_element_type=f32)
    panel = lax.dynamic_slice(prior, (my_group * slices, 0), (slices, groups * slices))
    coupled = jnp.einsum("ts,skn->tkn", panel, flux_all, precision=HI)
    w_recv = lax.all_to_all(
        w_send.reshape(n_source, cap * directions), "cell", split_axis=0, concat_axis=0, tiled=True
    ).reshape(n_slot, directions)

    hot_tt = meta_hot.reshape(n_slot, tiles, slices).transpose(0, 2, 1)
    w_meta = (hot_tt[:, :, None, :] * w_recv[:, None, :, None]).reshape(n_slot, n_meta * directions)
    adj = jnp.dot(w_meta.T, foot_r.astype(f32), precision=HI, preferred_element_type=f32)
    adjoint = adj.reshape(slices, directions, cell_count)

    hess = adjoint + coupled
    return (images, hess)


def solution(mesh):
    in_specs = (
        P("tm", None, "cell"),
        P("cell", "tm", None),
        P("cell", "tm"),
        P("cell", "tm"),
        P("cell", "tm"),
        P("cell", None, None),
        P("cell"),
        P(),
    )
    out_specs = (P("cell", None), P("tm", None, "cell"))
    return jax.shard_map(local, mesh=mesh, in_specs=in_specs, out_specs=out_specs, check_vma=False)
```

```python
import jax
import jax.numpy as jnp
from jax import lax
from jax.sharding import PartitionSpec as P

TILE = 128
HI = lax.Precision.HIGHEST


def local(flux, foot, block_slot, block_time, block_count, request_tiles, obs_weight, prior):
    slices, directions, cell_count = flux.shape
    tiles = cell_count // TILE
    sounds, nb, _ = foot.shape
    n_source = request_tiles.shape[1]
    per_source = request_tiles.shape[2]
    n_blocks = sounds * nb
    cap = 16
    n_slot = n_source * cap
    n_meta = tiles * slices
    f32 = jnp.float32

    live = (jnp.arange(nb, dtype=jnp.int32)[None, :] < block_count).reshape(n_blocks)
    slot_ids = block_slot.reshape(n_blocks)
    source = slot_ids // per_source
    position = slot_ids % per_source
    table = request_tiles[0].reshape(n_source * per_source)
    pick = slot_ids[:, None] == jnp.arange(n_source * per_source, dtype=jnp.int32)[None, :]
    local_tile = jnp.sum(jnp.where(pick, table[None, :], 0), axis=1)
    meta = local_tile * slices + block_time.reshape(n_blocks)
    src_hot = (source[:, None] == jnp.arange(n_source, dtype=jnp.int32)[None, :]) & live[:, None]
    src_hot_b = src_hot.astype(jnp.bfloat16)
    row = jnp.arange(n_blocks, dtype=jnp.int32)
    lower = (row[None, :] < row[:, None]).astype(jnp.bfloat16)
    before = jnp.dot(lower, src_hot_b, preferred_element_type=f32)
    rank = jnp.sum(before * src_hot_b.astype(f32), axis=1).astype(jnp.int32)
    dest = jnp.where(live, source * cap + rank, n_slot)
    place = (dest[None, :] == jnp.arange(n_slot, dtype=jnp.int32)[:, None])
    place_b = place.astype(jnp.bfloat16)
    foot_flat = foot.reshape(n_blocks, TILE)
    foot_send = jnp.dot(place_b, foot_flat, preferred_element_type=f32).astype(jnp.bfloat16)
    meta_send = jnp.sum(jnp.where(place, meta[None, :], 0), axis=1)
    meta_send = meta_send.reshape(n_source, cap).astype(jnp.bfloat16)
    meta_pad = jnp.zeros((n_source, TILE - cap), jnp.bfloat16)
    send = jnp.concatenate([foot_send.reshape(n_source, cap * TILE), meta_send, meta_pad], axis=1)
    send = send.reshape(n_source, 2, (cap + 1) * TILE // 2)
    recv = lax.all_to_all(send, "cell", split_axis=0, concat_axis=0, tiled=True)
    recv = recv.reshape(n_source, (cap + 1) * TILE)

    my_group = lax.axis_index("tm")
    groups = lax.axis_size("tm")
    foot_r = recv[:, : cap * TILE].reshape(n_slot, TILE)
    meta_r = recv[:, cap * TILE : cap * TILE + cap].reshape(n_slot).astype(jnp.int32)
    meta_hot = (meta_r[:, None] == jnp.arange(n_meta, dtype=jnp.int32)[None, :]).astype(f32)
    panels = flux.reshape(slices, directions, tiles, TILE).transpose(3, 2, 0, 1)
    panels = panels.reshape(TILE, n_meta * directions)
    every = jnp.dot(foot_r, panels, preferred_element_type=f32).reshape(n_slot, n_meta, directions)
    partial = jnp.sum(every * meta_hot[:, :, None], axis=1)
    back = lax.all_to_all(
        partial.reshape(n_source, cap * directions), "cell", split_axis=0, concat_axis=0, tiled=True
    ).reshape(n_slot, directions)

    place_f = place.astype(f32)
    per_block = jnp.dot(place_f.T, back, precision=HI, preferred_element_type=f32)
    partial_value = per_block.reshape(sounds, nb, directions).sum(axis=1)
    bf = jnp.bfloat16
    hi = lax.reduce_precision(partial_value, exponent_bits=8, mantissa_bits=7)
    rest = partial_value - hi
    mid = lax.reduce_precision(rest, exponent_bits=8, mantissa_bits=7)
    lo = rest - mid
    pieces = jnp.stack([hi, mid, lo]).astype(bf).reshape(-1, TILE)
    flux_rows = flux.reshape(-1, TILE)
    payload = jnp.concatenate([flux_rows, pieces], axis=0)
    copies = jnp.broadcast_to(payload[None], (groups,) + payload.shape)
    arrived = lax.all_to_all(copies, "tm", split_axis=0, concat_axis=0, tiled=True)
    n_rows = flux_rows.shape[0]
    flux_all = arrived[:, :n_rows].reshape(groups * slices, directions, cell_count).astype(f32)
    parts = arrived[:, n_rows:].reshape(groups, 3, sounds, directions).astype(f32)
    values = (parts[:, 0] + parts[:, 1]) + parts[:, 2]
    images = values.sum(axis=0)
    weighted = obs_weight[:, None] * images
    w_block = jnp.repeat(weighted, nb, axis=0)
    w_send = jnp.dot(place_f, w_block, precision=HI, preferred_element_type=f32)
    panel = lax.dynamic_slice(prior, (my_group * slices, 0), (slices, groups * slices))
    coupled = jnp.einsum("ts,skn->tkn", panel, flux_all, precision=HI)
    w_recv = lax.all_to_all(
        w_send.reshape(n_source, cap * directions), "cell", split_axis=0, concat_axis=0, tiled=True
    ).reshape(n_slot, directions)

    hot_tt = meta_hot.reshape(n_slot, tiles, slices).transpose(0, 2, 1)
    w_meta = (hot_tt[:, :, None, :] * w_recv[:, None, :, None]).reshape(n_slot, n_meta * directions)
    adj = jnp.dot(w_meta.T, foot_r.astype(f32), precision=HI, preferred_element_type=f32)
    adjoint = adj.reshape(slices, directions, cell_count)

    hess = adjoint + coupled
    return (images, hess)


def solution(mesh):
    in_specs = (
        P("tm", None, "cell"),
        P("cell", "tm", None),
        P("cell", "tm"),
        P("cell", "tm"),
        P("cell", "tm"),
        P("cell", None, None),
        P("cell"),
        P(),
    )
    out_specs = (P("cell", None), P("tm", None, "cell"))
    return jax.shard_map(local, mesh=mesh, in_specs=in_specs, out_specs=out_specs, check_vma=False)
```

```python
import jax
import jax.numpy as jnp
from jax import lax
from jax.sharding import PartitionSpec as P

TILE = 128
HI = lax.Precision.HIGHEST


def local(flux, foot, block_slot, block_time, block_count, request_tiles, obs_weight, prior):
    slices, directions, cell_count = flux.shape
    tiles = cell_count // TILE
    sounds, nb, _ = foot.shape
    n_source = request_tiles.shape[1]
    per_source = request_tiles.shape[2]
    n_blocks = sounds * nb
    cap = 16
    n_slot = n_source * cap
    n_meta = tiles * slices
    f32 = jnp.float32

    live = (jnp.arange(nb, dtype=jnp.int32)[None, :] < block_count).reshape(n_blocks)
    slot_ids = block_slot.reshape(n_blocks)
    source = slot_ids // per_source
    position = slot_ids % per_source
    table = request_tiles[0].reshape(n_source * per_source)
    pick = slot_ids[:, None] == jnp.arange(n_source * per_source, dtype=jnp.int32)[None, :]
    local_tile = jnp.sum(jnp.where(pick, table[None, :], 0), axis=1)
    meta = local_tile * slices + block_time.reshape(n_blocks)
    src_hot = (source[:, None] == jnp.arange(n_source, dtype=jnp.int32)[None, :]) & live[:, None]
    src_hot_b = src_hot.astype(jnp.bfloat16)
    row = jnp.arange(n_blocks, dtype=jnp.int32)
    lower = (row[None, :] < row[:, None]).astype(jnp.bfloat16)
    before = jnp.dot(lower, src_hot_b, preferred_element_type=f32)
    rank = jnp.sum(before * src_hot_b.astype(f32), axis=1).astype(jnp.int32)
    dest = jnp.where(live, source * cap + rank, n_slot)
    place = (dest[None, :] == jnp.arange(n_slot, dtype=jnp.int32)[:, None])
    place_b = place.astype(jnp.bfloat16)
    foot_flat = foot.reshape(n_blocks, TILE)
    foot_send = jnp.dot(place_b, foot_flat, preferred_element_type=f32).astype(jnp.bfloat16)
    meta_send = jnp.sum(jnp.where(place, meta[None, :], 0), axis=1)
    meta_send = meta_send.reshape(n_source, cap).astype(jnp.bfloat16)
    meta_pad = jnp.zeros((n_source, TILE - cap), jnp.bfloat16)
    send = jnp.concatenate([foot_send.reshape(n_source, cap * TILE), meta_send, meta_pad], axis=1)
    send = send.reshape(n_source, 2, (cap + 1) * TILE // 2)
    recv = lax.all_to_all(send, "cell", split_axis=0, concat_axis=0, tiled=True)
    recv = recv.reshape(n_source, (cap + 1) * TILE)

    my_group = lax.axis_index("tm")
    groups = lax.axis_size("tm")
    foot_r = recv[:, : cap * TILE].reshape(n_slot, TILE)
    meta_r = recv[:, cap * TILE : cap * TILE + cap].reshape(n_slot).astype(jnp.int32)
    meta_hot = (meta_r[:, None] == jnp.arange(n_meta, dtype=jnp.int32)[None, :]).astype(f32)
    panels = flux.reshape(slices, directions, tiles, TILE).transpose(3, 2, 0, 1)
    panels = panels.reshape(TILE, n_meta * directions)
    every = jnp.dot(foot_r, panels, preferred_element_type=f32).reshape(n_slot, n_meta, directions)
    partial = jnp.sum(every * meta_hot[:, :, None], axis=1)
    back = lax.all_to_all(
        partial.reshape(n_source, 2, cap * directions // 2), "cell", split_axis=0, concat_axis=0, tiled=True
    ).reshape(n_slot, directions)

    place_f = place.astype(f32)
    per_block = jnp.dot(place_f.T, back, precision=HI, preferred_element_type=f32)
    partial_value = per_block.reshape(sounds, nb, directions).sum(axis=1)
    bf = jnp.bfloat16
    hi = lax.reduce_precision(partial_value, exponent_bits=8, mantissa_bits=7)
    rest = partial_value - hi
    mid = lax.reduce_precision(rest, exponent_bits=8, mantissa_bits=7)
    lo = rest - mid
    pieces = jnp.stack([hi, mid, lo]).astype(bf).reshape(-1, TILE)
    flux_rows = flux.reshape(-1, TILE)
    payload = jnp.concatenate([flux_rows, pieces], axis=0)
    copies = jnp.broadcast_to(payload[None], (groups,) + payload.shape)
    arrived = lax.all_to_all(copies, "tm", split_axis=0, concat_axis=0, tiled=True)
    n_rows = flux_rows.shape[0]
    flux_all = arrived[:, :n_rows].reshape(groups * slices, directions, cell_count).astype(f32)
    parts = arrived[:, n_rows:].reshape(groups, 3, sounds, directions).astype(f32)
    values = (parts[:, 0] + parts[:, 1]) + parts[:, 2]
    images = values.sum(axis=0)
    weighted = obs_weight[:, None] * images
    w_block = jnp.repeat(weighted, nb, axis=0)
    w_send = jnp.dot(place_f, w_block, precision=HI, preferred_element_type=f32)
    panel = lax.dynamic_slice(prior, (my_group * slices, 0), (slices, groups * slices))
    coupled = jnp.einsum("ts,skn->tkn", panel, flux_all, precision=HI)
    w_recv = lax.all_to_all(
        w_send.reshape(n_source, 2, cap * directions // 2), "cell", split_axis=0, concat_axis=0, tiled=True
    ).reshape(n_slot, directions)

    hot_tt = meta_hot.reshape(n_slot, tiles, slices).transpose(0, 2, 1)
    w_meta = (hot_tt[:, :, None, :] * w_recv[:, None, :, None]).reshape(n_slot, n_meta * directions)
    adj = jnp.dot(w_meta.T, foot_r.astype(f32), precision=HI, preferred_element_type=f32)
    adjoint = adj.reshape(slices, directions, cell_count)

    hess = adjoint + coupled
    return (images, hess)


def solution(mesh):
    in_specs = (
        P("tm", None, "cell"),
        P("cell", "tm", None),
        P("cell", "tm"),
        P("cell", "tm"),
        P("cell", "tm"),
        P("cell", None, None),
        P("cell"),
        P(),
    )
    out_specs = (P("cell", None), P("tm", None, "cell"))
    return jax.shard_map(local, mesh=mesh, in_specs=in_specs, out_specs=out_specs, check_vma=False)
```

```python
import jax
import jax.numpy as jnp
from jax import lax
from jax.sharding import PartitionSpec as P

TILE = 128
HI = lax.Precision.HIGHEST


def local(flux, foot, block_slot, block_time, block_count, request_tiles, obs_weight, prior):
    slices, directions, cell_count = flux.shape
    tiles = cell_count // TILE
    sounds, nb, _ = foot.shape
    n_source = request_tiles.shape[1]
    per_source = request_tiles.shape[2]
    n_blocks = sounds * nb
    cap = 16
    n_slot = n_source * cap
    n_meta = tiles * slices
    f32 = jnp.float32

    live = (jnp.arange(nb, dtype=jnp.int32)[None, :] < block_count).reshape(n_blocks)
    slot_ids = block_slot.reshape(n_blocks)
    source = slot_ids // per_source
    position = slot_ids % per_source
    table = request_tiles[0]
    chosen = jnp.where(position[:, None] == 0, table[None, :, 0], table[None, :, per_source - 1])
    pick = source[:, None] == jnp.arange(n_source, dtype=jnp.int32)[None, :]
    local_tile = jnp.sum(jnp.where(pick, chosen, 0), axis=1)
    meta = local_tile * slices + block_time.reshape(n_blocks)
    src_hot = (source[:, None] == jnp.arange(n_source, dtype=jnp.int32)[None, :]) & live[:, None]
    src_hot_b = src_hot.astype(jnp.bfloat16)
    row = jnp.arange(n_blocks, dtype=jnp.int32)
    lower = (row[None, :] < row[:, None]).astype(jnp.bfloat16)
    before = jnp.dot(lower, src_hot_b, preferred_element_type=f32)
    rank = jnp.sum(before * src_hot_b.astype(f32), axis=1).astype(jnp.int32)
    dest = jnp.where(live, source * cap + rank, n_slot)
    place = (dest[None, :] == jnp.arange(n_slot, dtype=jnp.int32)[:, None])
    place_b = place.astype(jnp.bfloat16)
    foot_flat = foot.reshape(n_blocks, TILE)
    foot_send = jnp.dot(place_b, foot_flat, preferred_element_type=f32).astype(jnp.bfloat16)
    meta_send = jnp.sum(jnp.where(place, meta[None, :], 0), axis=1)
    meta_send = meta_send.reshape(n_source, cap).astype(jnp.bfloat16)
    meta_pad = jnp.zeros((n_source, TILE - cap), jnp.bfloat16)
    send = jnp.concatenate([foot_send.reshape(n_source, cap * TILE), meta_send, meta_pad], axis=1)
    send = send.reshape(n_source, 2, (cap + 1) * TILE // 2)
    recv = lax.all_to_all(send, "cell", split_axis=0, concat_axis=0, tiled=True)
    recv = recv.reshape(n_source, (cap + 1) * TILE)

    my_group = lax.axis_index("tm")
    groups = lax.axis_size("tm")
    foot_r = recv[:, : cap * TILE].reshape(n_slot, TILE)
    meta_r = recv[:, cap * TILE : cap * TILE + cap].reshape(n_slot).astype(jnp.int32)
    meta_hot = (meta_r[:, None] == jnp.arange(n_meta, dtype=jnp.int32)[None, :]).astype(f32)
    panels = flux.reshape(slices, directions, tiles, TILE).transpose(3, 2, 0, 1)
    panels = panels.reshape(TILE, n_meta * directions)
    every = jnp.dot(foot_r, panels, preferred_element_type=f32).reshape(n_slot, n_meta, directions)
    partial = jnp.sum(every * meta_hot[:, :, None], axis=1)
    back = lax.all_to_all(
        partial.reshape(n_source, 2, cap * directions // 2), "cell", split_axis=0, concat_axis=0, tiled=True
    ).reshape(n_slot, directions)

    place_f = place.astype(f32)
    per_block = jnp.dot(place_f.T, back, precision=HI, preferred_element_type=f32)
    partial_value = per_block.reshape(sounds, nb, directions).sum(axis=1)
    bf = jnp.bfloat16
    hi = lax.reduce_precision(partial_value, exponent_bits=8, mantissa_bits=7)
    rest = partial_value - hi
    mid = lax.reduce_precision(rest, exponent_bits=8, mantissa_bits=7)
    lo = rest - mid
    pieces = jnp.stack([hi, mid, lo]).astype(bf).reshape(-1, TILE)
    flux_rows = flux.reshape(-1, TILE)
    payload = jnp.concatenate([flux_rows, pieces], axis=0)
    copies = jnp.broadcast_to(payload[None], (groups,) + payload.shape)
    arrived = lax.all_to_all(copies, "tm", split_axis=0, concat_axis=0, tiled=True)
    n_rows = flux_rows.shape[0]
    flux_all = arrived[:, :n_rows].reshape(groups * slices, directions, cell_count).astype(f32)
    parts = arrived[:, n_rows:].reshape(groups, 3, sounds, directions).astype(f32)
    values = (parts[:, 0] + parts[:, 1]) + parts[:, 2]
    images = values.sum(axis=0)
    weighted = obs_weight[:, None] * images
    w_block = jnp.repeat(weighted, nb, axis=0)
    w_send = jnp.dot(place_f, w_block, precision=HI, preferred_element_type=f32)
    panel = lax.dynamic_slice(prior, (my_group * slices, 0), (slices, groups * slices))
    coupled = jnp.einsum("ts,skn->tkn", panel, flux_all, precision=HI)
    w_recv = lax.all_to_all(
        w_send.reshape(n_source, 2, cap * directions // 2), "cell", split_axis=0, concat_axis=0, tiled=True
    ).reshape(n_slot, directions)

    hot_tt = meta_hot.reshape(n_slot, tiles, slices).transpose(0, 2, 1)
    w_meta = (hot_tt[:, :, None, :] * w_recv[:, None, :, None]).reshape(n_slot, n_meta * directions)
    adj = jnp.dot(w_meta.T, foot_r.astype(f32), precision=HI, preferred_element_type=f32)
    adjoint = adj.reshape(slices, directions, cell_count)

    hess = adjoint + coupled
    return (images, hess)


def solution(mesh):
    in_specs = (
        P("tm", None, "cell"),
        P("cell", "tm", None),
        P("cell", "tm"),
        P("cell", "tm"),
        P("cell", "tm"),
        P("cell", None, None),
        P("cell"),
        P(),
    )
    out_specs = (P("cell", None), P("tm", None, "cell"))
    return jax.shard_map(local, mesh=mesh, in_specs=in_specs, out_specs=out_specs, check_vma=False)
```

```python
import jax
import jax.numpy as jnp
from jax import lax
from jax.sharding import PartitionSpec as P

TILE = 128
HI = lax.Precision.HIGHEST


def local(flux, foot, block_slot, block_time, block_count, request_tiles, obs_weight, prior):
    slices, directions, cell_count = flux.shape
    tiles = cell_count // TILE
    sounds, nb, _ = foot.shape
    n_source = request_tiles.shape[1]
    per_source = request_tiles.shape[2]
    n_blocks = sounds * nb
    cap = 16
    n_slot = n_source * cap
    n_meta = tiles * slices
    f32 = jnp.float32

    live = (jnp.arange(nb, dtype=jnp.int32)[None, :] < block_count).reshape(n_blocks)
    slot_ids = block_slot.reshape(n_blocks)
    source = slot_ids // per_source
    position = slot_ids % per_source
    table = request_tiles[0]
    chosen = jnp.where(position[:, None] == 0, table[None, :, 0], table[None, :, per_source - 1])
    pick = source[:, None] == jnp.arange(n_source, dtype=jnp.int32)[None, :]
    local_tile = jnp.sum(jnp.where(pick, chosen, 0), axis=1)
    meta = (local_tile.reshape(sounds, nb) * slices + block_time).reshape(n_blocks)
    src_hot = (source[:, None] == jnp.arange(n_source, dtype=jnp.int32)[None, :]) & live[:, None]
    src_hot_b = src_hot.astype(jnp.bfloat16)
    row = jnp.arange(n_blocks, dtype=jnp.int32)
    lower = (row[None, :] < row[:, None]).astype(jnp.bfloat16)
    before = jnp.dot(lower, src_hot_b, preferred_element_type=f32)
    rank = jnp.sum(before * src_hot_b.astype(f32), axis=1).astype(jnp.int32)
    dest = jnp.where(live, source * cap + rank, n_slot)
    place = (dest[None, :] == jnp.arange(n_slot, dtype=jnp.int32)[:, None])
    place_b = place.astype(jnp.bfloat16)
    foot_flat = foot.reshape(n_blocks, TILE)
    foot_send = jnp.dot(place_b, foot_flat, preferred_element_type=f32).astype(jnp.bfloat16)
    meta_send = jnp.sum(jnp.where(place, meta[None, :], 0), axis=1)
    meta_send = meta_send.reshape(n_source, cap).astype(jnp.bfloat16)
    meta_pad = jnp.zeros((n_source, TILE - cap), jnp.bfloat16)
    send = jnp.concatenate([foot_send.reshape(n_source, cap * TILE), meta_send, meta_pad], axis=1)
    send = send.reshape(n_source, 2, (cap + 1) * TILE // 2)
    recv = lax.all_to_all(send, "cell", split_axis=0, concat_axis=0, tiled=True)
    recv = recv.reshape(n_source, (cap + 1) * TILE)

    my_group = lax.axis_index("tm")
    groups = lax.axis_size("tm")
    foot_r = recv[:, : cap * TILE].reshape(n_slot, TILE)
    meta_r = recv[:, cap * TILE : cap * TILE + cap].reshape(n_slot).astype(jnp.int32)
    meta_hot = (meta_r[:, None] == jnp.arange(n_meta, dtype=jnp.int32)[None, :]).astype(f32)
    panels = flux.reshape(slices, directions, tiles, TILE).transpose(3, 2, 0, 1)
    panels = panels.reshape(TILE, n_meta * directions)
    every = jnp.dot(foot_r, panels, preferred_element_type=f32).reshape(n_slot, n_meta, directions)
    partial = jnp.sum(every * meta_hot[:, :, None], axis=1)
    back = lax.all_to_all(
        partial.reshape(n_source, 2, cap * directions // 2), "cell", split_axis=0, concat_axis=0, tiled=True
    ).reshape(n_slot, directions)

    place_f = place.astype(f32)
    per_block = jnp.dot(place_f.T, back, precision=HI, preferred_element_type=f32)
    partial_value = per_block.reshape(sounds, nb, directions).sum(axis=1)
    bf = jnp.bfloat16
    hi = lax.reduce_precision(partial_value, exponent_bits=8, mantissa_bits=7)
    rest = partial_value - hi
    mid = lax.reduce_precision(rest, exponent_bits=8, mantissa_bits=7)
    lo = rest - mid
    pieces = jnp.stack([hi, mid, lo]).astype(bf).reshape(-1, TILE)
    flux_rows = flux.reshape(-1, TILE)
    payload = jnp.concatenate([flux_rows, pieces], axis=0)
    copies = jnp.broadcast_to(payload[None], (groups,) + payload.shape)
    arrived = lax.all_to_all(copies, "tm", split_axis=0, concat_axis=0, tiled=True)
    n_rows = flux_rows.shape[0]
    flux_all = arrived[:, :n_rows].reshape(groups * slices, directions, cell_count).astype(f32)
    parts = arrived[:, n_rows:].reshape(groups, 3, sounds, directions).astype(f32)
    values = (parts[:, 0] + parts[:, 1]) + parts[:, 2]
    images = values.sum(axis=0)
    weighted = obs_weight[:, None] * images
    w_block = jnp.repeat(weighted, nb, axis=0)
    w_send = jnp.dot(place_f, w_block, precision=HI, preferred_element_type=f32)
    panel = lax.dynamic_slice(prior, (my_group * slices, 0), (slices, groups * slices))
    coupled = jnp.einsum("ts,skn->tkn", panel, flux_all, precision=HI)
    w_recv = lax.all_to_all(
        w_send.reshape(n_source, 2, cap * directions // 2), "cell", split_axis=0, concat_axis=0, tiled=True
    ).reshape(n_slot, directions)

    hot_tt = meta_hot.reshape(n_slot, tiles, slices).transpose(0, 2, 1)
    w_meta = (hot_tt[:, :, None, :] * w_recv[:, None, :, None]).reshape(n_slot, n_meta * directions)
    adj = jnp.dot(w_meta.T, foot_r.astype(f32), precision=HI, preferred_element_type=f32)
    adjoint = adj.reshape(slices, directions, cell_count)

    hess = adjoint + coupled
    return (images, hess)


def solution(mesh):
    in_specs = (
        P("tm", None, "cell"),
        P("cell", "tm", None),
        P("cell", "tm"),
        P("cell", "tm"),
        P("cell", "tm"),
        P("cell", None, None),
        P("cell"),
        P(),
    )
    out_specs = (P("cell", None), P("tm", None, "cell"))
    return jax.shard_map(local, mesh=mesh, in_specs=in_specs, out_specs=out_specs, check_vma=False)
```
